32 devices in a mesh: mp: 2 (over y), tx: 4 (over z), ty: 4 (over x, core).
Axes of the slice: x: 2, y: 2, z: 4, core: 2. Of those that a mesh axis runs over, the one named last changes fastest.
Arguments:
- models: float32 [2, 16, 64, 512], P('mp', None, 'ty', 'tx'), may hold values from -6 to 6
- direction: float32 [2, 16, 64, 512], P('mp', None, 'ty', 'tx'), may hold values from -6 to 6
- coupling: float32 [2], replicated, may hold values from 0.1 to 0.4
- tv_weight: float32 [2], replicated, may hold values from 0.5 to 2
Outputs:
- gradient: float32 [2, 16, 64, 512], P('mp', None, 'ty', 'tx')
- hessian_vector: float32 [2, 16, 64, 512], P('mp', None, 'ty', 'tx')
The draws below stay inside these ranges and needn't reach their ends.
All inputs are finite; a program needn't handle non-finite values.
Results may differ from the reference program's by a relative error of at most 0.0001.
Values sent between devices are 32-bit elements; how exact they have to be, the bound alone decides.
No kernel may reach another device: no remote copies, remote signals or barrier semaphores. Data moves between devices by JAX's collectives and lax.ppermute only.
A program may use at most 64 MiB of HBM per device.

```python
import math
import jax
import jax.numpy as jnp
from jax import lax

NZ = 16
MODELS = 2
NX = 512
NY = 64


def block_levels(rng, extent, pieces, smallest, high):
    def one(dim, shards_of):
        heights = jax.random.uniform(jax.random.fold_in(jax.random.fold_in(rng, 6), dim), (shards_of,), jnp.float32, smallest / len(pieces), high / len(pieces))
        return jnp.repeat(jnp.exp(heights), extent[dim] // shards_of).reshape((-1,) + (1,) * (len(extent) - dim - 1))

    gain = one(*pieces[0])
    for cut in pieces[1:]:
        gain = gain * one(*cut)
    return gain


def scatter_about(stream_key, shape, spread, most, cuts=(), held_as=jnp.bfloat16):
    array = jax.random.normal(stream_key, shape, jnp.float32) * spread
    if len(cuts) > 0:
        array = block_levels(stream_key, shape, cuts, -0.22, 0.18) * array
    return jnp.clip(array, min=-most, max=most).astype(held_as)


def setup_inputs(seed: int = 0) -> dict:
    arg_keys = jax.random.split(jax.random.key(seed), 5)
    return {
        "models": scatter_about(arg_keys[0], (MODELS, NZ, NY, NX), 1.0, 6.0, ((0, 2), (2, 4), (3, 4)), jnp.float32),
        "direction": scatter_about(arg_keys[1], (MODELS, NZ, NY, NX), 1.0, 6.0, ((0, 2), (2, 4), (3, 4)), jnp.float32),
        "coupling": jnp.clip(jnp.exp(jax.random.uniform(arg_keys[2], (MODELS,), jnp.float32, math.log(0.1), math.log(0.4))), 0.1, 0.4),
        "tv_weight": jnp.clip(jnp.exp(jax.random.uniform(arg_keys[3], (MODELS,), jnp.float32, math.log(0.5), math.log(2.0))), 0.5, 2.0),
    }


EPS_SQ = 0.25
SYM_PAIRS = ((0, 0), (1, 1), (2, 2), (0, 1), (0, 2), (1, 2))

def forward_diffs(field):
    dx = jnp.concatenate([field[..., 1:] - field[..., :-1], jnp.zeros_like(field[..., :1])], -1)
    dy = jnp.concatenate([field[..., 1:, :] - field[..., :-1, :], jnp.zeros_like(field[..., :1, :])], -2)
    dz = jnp.concatenate([field[..., 1:, :, :] - field[..., :-1, :, :], jnp.zeros_like(field[..., :1, :, :])], -3)
    return jnp.stack([dx, dy, dz], axis=-4)

def adjoint(flux):
    fx = flux[..., 0, :, :, :]
    fy = flux[..., 1, :, :, :]
    fz = flux[..., 2, :, :, :]
    mx = jnp.concatenate([fx[..., :-1], jnp.zeros_like(fx[..., :1])], -1)
    my = jnp.concatenate([fy[..., :-1, :], jnp.zeros_like(fy[..., :1, :])], -2)
    mz = jnp.concatenate([fz[..., :-1, :, :], jnp.zeros_like(fz[..., :1, :, :])], -3)
    res = jnp.concatenate([jnp.zeros_like(fx[..., :1]), mx[..., :-1]], -1) - mx
    res = res + jnp.concatenate([jnp.zeros_like(fy[..., :1, :]), my[..., :-1, :]], -2) - my
    res = res + jnp.concatenate([jnp.zeros_like(fz[..., :1, :, :]), mz[..., :-1, :, :]], -3) - mz
    return res

def moments(grads, dirs, weights):
    wts = weights[:, None, None, None]
    rows = [lax.optimization_barrier(jnp.sum(wts * grads[:, i] * grads[:, j], 0)) for i, j in SYM_PAIRS]
    for i in range(3):
        for j in range(3):
            rows.append(lax.optimization_barrier(jnp.sum(wts * dirs[:, i] * grads[:, j], 0)))
    return jnp.stack(rows, 0)

def couple(moms, grad_own, dir_own):
    trace_m = moms[0] + moms[1] + moms[2]
    mat = [[moms[0], moms[3], moms[4]], [moms[3], moms[1], moms[5]], [moms[4], moms[5], moms[2]]]
    nat = [[moms[6 + 3 * i + j] for j in range(3)] for i in range(3)]
    trace_n = nat[0][0] + nat[1][1] + nat[2][2]
    g_parts = [grad_own[..., i, :, :, :] for i in range(3)]
    e_parts = [dir_own[..., i, :, :, :] for i in range(3)]
    cross_q = []
    cross_p = []
    for i in range(3):
        mg = mat[i][0] * g_parts[0] + mat[i][1] * g_parts[1] + mat[i][2] * g_parts[2]
        me = mat[i][0] * e_parts[0] + mat[i][1] * e_parts[1] + mat[i][2] * e_parts[2]
        ng = nat[i][0] * g_parts[0] + nat[i][1] * g_parts[1] + nat[i][2] * g_parts[2]
        cross_q.append(trace_m * g_parts[i] - mg)
        cross_p.append(trace_m * e_parts[i] - me + trace_n * g_parts[i] - ng)
    return (jnp.stack(cross_q, axis=-4), jnp.stack(cross_p, axis=-4))

def reference(models, direction, coupling, tv_weight):
    grads = forward_diffs(models)
    dirs = forward_diffs(direction)
    moms = moments(grads, dirs, coupling)
    cross_q, cross_p = couple(moms, grads, dirs)
    size = jnp.sqrt(lax.optimization_barrier(jnp.sum(grads * grads, 1)) + EPS_SQ)[:, None]
    alpha = coupling[:, None, None, None, None]
    beta = tv_weight[:, None, None, None, None]
    gradient = adjoint(beta * grads / size + alpha * cross_q)
    hessian_vector = adjoint(beta * dirs / size + alpha * cross_p)
    return (gradient, hessian_vector)
```

```python
import jax
import jax.numpy as jnp
from jax import lax
from jax.sharding import PartitionSpec as P

EPS_SQ = 0.25
SYM_PAIRS = ((0, 0), (1, 1), (2, 2), (0, 1), (0, 2), (1, 2))


def passed_along(array, axis, by):
    size = lax.axis_size(axis)
    pairs = [(i, i + by) for i in range(size) if 0 <= i + by < size]
    return lax.ppermute(array, axis, pairs)


def edge_masks(width_y, width_x):
    end_x = lax.axis_index("tx") == lax.axis_size("tx") - 1
    end_y = lax.axis_index("ty") == lax.axis_size("ty") - 1
    col_x = lax.broadcasted_iota(jnp.int32, (1, 1, width_x), 2)
    row_y = lax.broadcasted_iota(jnp.int32, (1, width_y, 1), 1)
    return ((col_x == width_x - 1) & end_x, (row_y == width_y - 1) & end_y)


def fields(tile, rim_x, rim_y):
    last_x, last_y = edge_masks(tile.shape[3], tile.shape[4])
    dx = jnp.concatenate([tile[..., 1:], rim_x], -1) - tile
    dx = jnp.where(last_x, 0.0, dx)
    dy = jnp.concatenate([tile[..., 1:, :], rim_y], -2) - tile
    dy = jnp.where(last_y, 0.0, dy)
    dz = jnp.concatenate(
        [tile[..., 1:, :, :] - tile[..., :-1, :, :], jnp.zeros_like(tile[..., :1, :, :])], -3
    )
    grads = jnp.stack([dx[:, 0], dy[:, 0], dz[:, 0]], 1)
    dirs = jnp.stack([dx[:, 1], dy[:, 1], dz[:, 1]], 1)
    return (grads, dirs)


def moments(grads, dirs, weights):
    wts = weights[:, None, None, None]
    rows = [jnp.sum(wts * grads[:, i] * grads[:, j], 0) for i, j in SYM_PAIRS]
    for i in range(3):
        for j in range(3):
            rows.append(jnp.sum(wts * dirs[:, i] * grads[:, j], 0))
    return jnp.stack(rows, 0)


def couple(moms, grad_own, dir_own):
    trace_m = moms[0] + moms[1] + moms[2]
    mat = [[moms[0], moms[3], moms[4]], [moms[3], moms[1], moms[5]], [moms[4], moms[5], moms[2]]]
    nat = [[moms[6 + 3 * i + j] for j in range(3)] for i in range(3)]
    trace_n = nat[0][0] + nat[1][1] + nat[2][2]
    g_parts = [grad_own[..., i, :, :, :] for i in range(3)]
    e_parts = [dir_own[..., i, :, :, :] for i in range(3)]
    cross_q = []
    cross_p = []
    for i in range(3):
        mg = mat[i][0] * g_parts[0] + mat[i][1] * g_parts[1] + mat[i][2] * g_parts[2]
        me = mat[i][0] * e_parts[0] + mat[i][1] * e_parts[1] + mat[i][2] * e_parts[2]
        ng = nat[i][0] * g_parts[0] + nat[i][1] * g_parts[1] + nat[i][2] * g_parts[2]
        cross_q.append(trace_m * g_parts[i] - mg)
        cross_p.append(trace_m * e_parts[i] - me + trace_n * g_parts[i] - ng)
    return (jnp.stack(cross_q, axis=-4), jnp.stack(cross_p, axis=-4))


def model_split(every, rim_x, rim_y, alpha, beta, weights):
    grads, dirs = fields(every, rim_x, rim_y)
    moms = moments(grads, dirs, weights)
    grad_own = grads[0]
    dir_own = dirs[0]
    cross_q, cross_p = couple(moms, grad_own, dir_own)
    size = jnp.sqrt(jnp.sum(grad_own * grad_own, 0) + EPS_SQ)[None]
    flux = jnp.stack(
        [beta * grad_own / size + alpha * cross_q, beta * dir_own / size + alpha * cross_p], 0
    )
    last_x, last_y = edge_masks(flux.shape[3], flux.shape[4])
    flux_x = jnp.where(last_x, 0.0, flux[:, 0])
    flux_y = jnp.where(last_y, 0.0, flux[:, 1])
    flux_z = flux[:, 2]
    flux_z = jnp.concatenate([flux_z[..., :-1, :, :], jnp.zeros_like(flux_z[..., :1, :, :])], -3)
    prev_x = passed_along(flux_x[..., -1:], "tx", 1)
    prev_y = passed_along(flux_y[..., -1:, :], "ty", 1)
    result = jnp.concatenate([prev_x, flux_x[..., :-1]], -1) - flux_x
    result = result + jnp.concatenate([prev_y, flux_y[..., :-1, :]], -2) - flux_y
    result = (
        result
        + jnp.concatenate([jnp.zeros_like(flux_z[..., :1, :, :]), flux_z[..., :-1, :, :]], -3)
        - flux_z
    )
    return (result[0][None], result[1][None])


def rim_from(array, axis, shift):
    if shift == 0:
        return passed_along(array, axis, -1)
    mp = lax.axis_size("mp")
    size = lax.axis_size(axis)
    pairs = [
        (m * size + t, ((m + shift) % mp) * size + t - 1)
        for m in range(mp)
        for t in range(1, size)
    ]
    return lax.ppermute(array, ("mp", axis), pairs)


def shards(models, direction, coupling, tv_weight):
    mp = lax.axis_size("mp")
    member = lax.axis_index("mp")
    local = models.shape[0]
    own_weights = lax.dynamic_slice_in_dim(coupling, member * local, local)
    alpha = own_weights[0]
    beta = lax.dynamic_slice_in_dim(tv_weight, member * local, local)[0]
    own = jnp.stack([models, direction], 1)
    tiles, rims_x, rims_y, weights = [], [], [], []
    for shift in range(mp):
        if shift == 0:
            tiles.append(own)
        else:
            tiles.append(lax.ppermute(own, "mp", [(m, (m + shift) % mp) for m in range(mp)]))
        rims_x.append(rim_from(own[..., :1], "tx", shift))
        rims_y.append(rim_from(own[..., :1, :], "ty", shift))
        source = (member - shift) % mp
        weights.append(lax.dynamic_slice_in_dim(coupling, source * local, local))
    every = jnp.concatenate(tiles, 0)
    rim_x = jnp.concatenate(rims_x, 0)
    rim_y = jnp.concatenate(rims_y, 0)
    return model_split(every, rim_x, rim_y, alpha, beta, jnp.concatenate(weights, 0))


def solution(mesh):
    placed = (P("mp", None, "ty", "tx"), P("mp", None, "ty", "tx"), P(), P())
    return jax.shard_map(
        shards,
        mesh=mesh,
        in_specs=placed,
        out_specs=(P("mp", None, "ty", "tx"), P("mp", None, "ty", "tx")),
        check_vma=False,
    )
```

```python
import jax
import jax.numpy as jnp
from jax import lax
from jax.sharding import PartitionSpec as P

EPS_SQ = 0.25
SYM_PAIRS = ((0, 0), (1, 1), (2, 2), (0, 1), (0, 2), (1, 2))


def passed_along(array, axis, by):
    size = lax.axis_size(axis)
    pairs = [(i, i + by) for i in range(size) if 0 <= i + by < size]
    return lax.ppermute(array, axis, pairs)


def edge_masks(width_y, width_x):
    end_x = lax.axis_index("tx") == lax.axis_size("tx") - 1
    end_y = lax.axis_index("ty") == lax.axis_size("ty") - 1
    col_x = lax.broadcasted_iota(jnp.int32, (1, 1, width_x), 2)
    row_y = lax.broadcasted_iota(jnp.int32, (1, width_y, 1), 1)
    return ((col_x == width_x - 1) & end_x, (row_y == width_y - 1) & end_y)


def fields(tile, rim_x, rim_y):
    last_x, last_y = edge_masks(tile.shape[3], tile.shape[4])
    dx = jnp.concatenate([tile[..., 1:], rim_x], -1) - tile
    dx = jnp.where(last_x, 0.0, dx)
    dy = jnp.concatenate([tile[..., 1:, :], rim_y], -2) - tile
    dy = jnp.where(last_y, 0.0, dy)
    dz = jnp.concatenate(
        [tile[..., 1:, :, :] - tile[..., :-1, :, :], jnp.zeros_like(tile[..., :1, :, :])], -3
    )
    grads = jnp.stack([dx[:, 0], dy[:, 0], dz[:, 0]], 1)
    dirs = jnp.stack([dx[:, 1], dy[:, 1], dz[:, 1]], 1)
    return (grads, dirs)


def moments(grads, dirs, weights):
    wts = weights[:, None, None, None]
    rows = [jnp.sum(wts * grads[:, i] * grads[:, j], 0) for i, j in SYM_PAIRS]
    for i in range(3):
        for j in range(3):
            rows.append(jnp.sum(wts * dirs[:, i] * grads[:, j], 0))
    return jnp.stack(rows, 0)


def couple(moms, grad_own, dir_own):
    trace_m = moms[0] + moms[1] + moms[2]
    mat = [[moms[0], moms[3], moms[4]], [moms[3], moms[1], moms[5]], [moms[4], moms[5], moms[2]]]
    nat = [[moms[6 + 3 * i + j] for j in range(3)] for i in range(3)]
    trace_n = nat[0][0] + nat[1][1] + nat[2][2]
    g_parts = [grad_own[..., i, :, :, :] for i in range(3)]
    e_parts = [dir_own[..., i, :, :, :] for i in range(3)]
    cross_q = []
    cross_p = []
    for i in range(3):
        mg = mat[i][0] * g_parts[0] + mat[i][1] * g_parts[1] + mat[i][2] * g_parts[2]
        me = mat[i][0] * e_parts[0] + mat[i][1] * e_parts[1] + mat[i][2] * e_parts[2]
        ng = nat[i][0] * g_parts[0] + nat[i][1] * g_parts[1] + nat[i][2] * g_parts[2]
        cross_q.append(trace_m * g_parts[i] - mg)
        cross_p.append(trace_m * e_parts[i] - me + trace_n * g_parts[i] - ng)
    return (jnp.stack(cross_q, axis=-4), jnp.stack(cross_p, axis=-4))


def model_split(every, rim_x, rim_y, alpha, beta, weights):
    grads, dirs = fields(every, rim_x, rim_y)
    moms = moments(grads, dirs, weights)
    grad_own = grads[0]
    dir_own = dirs[0]
    cross_q, cross_p = couple(moms, grad_own, dir_own)
    size = jnp.sqrt(jnp.sum(grad_own * grad_own, 0) + EPS_SQ)[None]
    flux = jnp.stack(
        [beta * grad_own / size + alpha * cross_q, beta * dir_own / size + alpha * cross_p], 0
    )
    last_x, last_y = edge_masks(flux.shape[3], flux.shape[4])
    flux_x = jnp.where(last_x, 0.0, flux[:, 0])
    flux_y = jnp.where(last_y, 0.0, flux[:, 1])
    flux_z = flux[:, 2]
    flux_z = jnp.concatenate([flux_z[..., :-1, :, :], jnp.zeros_like(flux_z[..., :1, :, :])], -3)
    prev_x = passed_along(flux_x[..., -1:], "tx", 1)
    prev_y = passed_along(flux_y[..., -1:, :], "ty", 1)
    result = jnp.concatenate([prev_x, flux_x[..., :-1]], -1) - flux_x
    result = result + jnp.concatenate([prev_y, flux_y[..., :-1, :]], -2) - flux_y
    result = (
        result
        + jnp.concatenate([jnp.zeros_like(flux_z[..., :1, :, :]), flux_z[..., :-1, :, :]], -3)
        - flux_z
    )
    return (result[0][None], result[1][None])


def shards(models, direction, coupling, tv_weight):
    mp = lax.axis_size("mp")
    member = lax.axis_index("mp")
    local = models.shape[0]
    own_weights = lax.dynamic_slice_in_dim(coupling, member * local, local)
    alpha = own_weights[0]
    beta = lax.dynamic_slice_in_dim(tv_weight, member * local, local)[0]
    own = jnp.stack([models, direction], 1)
    tiles, weights = [own], [own_weights]
    for shift in range(1, mp):
        tiles.append(lax.ppermute(own, "mp", [(m, (m + shift) % mp) for m in range(mp)]))
        source = (member - shift) % mp
        weights.append(lax.dynamic_slice_in_dim(coupling, source * local, local))
    every = jnp.concatenate(tiles, 0)
    rim_x = passed_along(every[..., :1], "tx", -1)
    rim_y = passed_along(every[..., :1, :], "ty", -1)
    return model_split(every, rim_x, rim_y, alpha, beta, jnp.concatenate(weights, 0))


def solution(mesh):
    placed = (P("mp", None, "ty", "tx"), P("mp", None, "ty", "tx"), P(), P())
    return jax.shard_map(
        shards,
        mesh=mesh,
        in_specs=placed,
        out_specs=(P("mp", None, "ty", "tx"), P("mp", None, "ty", "tx")),
        check_vma=False,
    )
```

```python
import jax
import jax.numpy as jnp
from jax import lax
from jax.sharding import PartitionSpec as P

EPS_SQ = 0.25
SYM_PAIRS = ((0, 0), (1, 1), (2, 2), (0, 1), (0, 2), (1, 2))


def passed_along(array, axis, by):
    size = lax.axis_size(axis)
    pairs = [(i, i + by) for i in range(size) if 0 <= i + by < size]
    return lax.ppermute(array, axis, pairs)


def passed_dense(array, axis, by):
    count = array.size
    rows = array.reshape(count // 128, 128) if count % 128 == 0 else array.reshape(count)
    return passed_along(rows, axis, by).reshape(array.shape)


def edge_masks(width_y, width_x):
    end_x = lax.axis_index("tx") == lax.axis_size("tx") - 1
    end_y = lax.axis_index("ty") == lax.axis_size("ty") - 1
    col_x = lax.broadcasted_iota(jnp.int32, (1, 1, width_x), 2)
    row_y = lax.broadcasted_iota(jnp.int32, (1, width_y, 1), 1)
    return ((col_x == width_x - 1) & end_x, (row_y == width_y - 1) & end_y)


def fields(tile, rim_x, rim_y):
    last_x, last_y = edge_masks(tile.shape[3], tile.shape[4])
    dx = jnp.concatenate([tile[..., 1:], rim_x], -1) - tile
    dx = jnp.where(last_x, 0.0, dx)
    dy = jnp.concatenate([tile[..., 1:, :], rim_y], -2) - tile
    dy = jnp.where(last_y, 0.0, dy)
    dz = jnp.concatenate(
        [tile[..., 1:, :, :] - tile[..., :-1, :, :], jnp.zeros_like(tile[..., :1, :, :])], -3
    )
    grads = jnp.stack([dx[:, 0], dy[:, 0], dz[:, 0]], 1)
    dirs = jnp.stack([dx[:, 1], dy[:, 1], dz[:, 1]], 1)
    return (grads, dirs)


def moments(grads, dirs, weights):
    wts = weights[:, None, None, None]
    rows = [jnp.sum(wts * grads[:, i] * grads[:, j], 0) for i, j in SYM_PAIRS]
    for i in range(3):
        for j in range(3):
            rows.append(jnp.sum(wts * dirs[:, i] * grads[:, j], 0))
    return jnp.stack(rows, 0)


def couple(moms, grad_own, dir_own):
    trace_m = moms[0] + moms[1] + moms[2]
    mat = [[moms[0], moms[3], moms[4]], [moms[3], moms[1], moms[5]], [moms[4], moms[5], moms[2]]]
    nat = [[moms[6 + 3 * i + j] for j in range(3)] for i in range(3)]
    trace_n = nat[0][0] + nat[1][1] + nat[2][2]
    g_parts = [grad_own[..., i, :, :, :] for i in range(3)]
    e_parts = [dir_own[..., i, :, :, :] for i in range(3)]
    cross_q = []
    cross_p = []
    for i in range(3):
        mg = mat[i][0] * g_parts[0] + mat[i][1] * g_parts[1] + mat[i][2] * g_parts[2]
        me = mat[i][0] * e_parts[0] + mat[i][1] * e_parts[1] + mat[i][2] * e_parts[2]
        ng = nat[i][0] * g_parts[0] + nat[i][1] * g_parts[1] + nat[i][2] * g_parts[2]
        cross_q.append(trace_m * g_parts[i] - mg)
        cross_p.append(trace_m * e_parts[i] - me + trace_n * g_parts[i] - ng)
    return (jnp.stack(cross_q, axis=-4), jnp.stack(cross_p, axis=-4))


def model_split(every, rim_x, rim_y, alpha, beta, weights):
    grads, dirs = fields(every, rim_x, rim_y)
    moms = moments(grads, dirs, weights)
    grad_own = grads[0]
    dir_own = dirs[0]
    cross_q, cross_p = couple(moms, grad_own, dir_own)
    size = jnp.sqrt(jnp.sum(grad_own * grad_own, 0) + EPS_SQ)[None]
    flux = jnp.stack(
        [beta * grad_own / size + alpha * cross_q, beta * dir_own / size + alpha * cross_p], 0
    )
    last_x, last_y = edge_masks(flux.shape[3], flux.shape[4])
    flux_x = jnp.where(last_x, 0.0, flux[:, 0])
    flux_y = jnp.where(last_y, 0.0, flux[:, 1])
    flux_z = flux[:, 2]
    flux_z = jnp.concatenate([flux_z[..., :-1, :, :], jnp.zeros_like(flux_z[..., :1, :, :])], -3)
    prev_x = passed_dense(flux_x[..., -1:], "tx", 1)
    prev_y = passed_along(flux_y[..., -1:, :], "ty", 1)
    result = jnp.concatenate([prev_x, flux_x[..., :-1]], -1) - flux_x
    result = result + jnp.concatenate([prev_y, flux_y[..., :-1, :]], -2) - flux_y
    result = (
        result
        + jnp.concatenate([jnp.zeros_like(flux_z[..., :1, :, :]), flux_z[..., :-1, :, :]], -3)
        - flux_z
    )
    return (result[0][None], result[1][None])


def shards(models, direction, coupling, tv_weight):
    mp = lax.axis_size("mp")
    member = lax.axis_index("mp")
    local = models.shape[0]
    own_weights = lax.dynamic_slice_in_dim(coupling, member * local, local)
    alpha = own_weights[0]
    beta = lax.dynamic_slice_in_dim(tv_weight, member * local, local)[0]
    own = jnp.stack([models, direction], 1)
    tiles, weights = [own], [own_weights]
    for shift in range(1, mp):
        tiles.append(lax.ppermute(own, "mp", [(m, (m + shift) % mp) for m in range(mp)]))
        source = (member - shift) % mp
        weights.append(lax.dynamic_slice_in_dim(coupling, source * local, local))
    every = jnp.concatenate(tiles, 0)
    rim_x = passed_dense(every[..., :1], "tx", -1)
    rim_y = passed_along(every[..., :1, :], "ty", -1)
    return model_split(every, rim_x, rim_y, alpha, beta, jnp.concatenate(weights, 0))


def solution(mesh):
    placed = (P("mp", None, "ty", "tx"), P("mp", None, "ty", "tx"), P(), P())
    return jax.shard_map(
        shards,
        mesh=mesh,
        in_specs=placed,
        out_specs=(P("mp", None, "ty", "tx"), P("mp", None, "ty", "tx")),
        check_vma=False,
    )
```

```python
import jax
import jax.numpy as jnp
from jax import lax
from jax.sharding import PartitionSpec as P

EPS_SQ = 0.25
SYM_PAIRS = ((0, 0), (1, 1), (2, 2), (0, 1), (0, 2), (1, 2))


def passed_along(array, axis, by):
    size = lax.axis_size(axis)
    pairs = [(i, i + by) for i in range(size) if 0 <= i + by < size]
    return lax.ppermute(array, axis, pairs)


def passed_dense(array, axis, by):
    count = array.size
    rows = array.reshape(count // 128, 128) if count % 128 == 0 else array.reshape(count)
    return passed_along(rows, axis, by).reshape(array.shape)


def edge_masks(width_y, width_x):
    end_x = lax.axis_index("tx") == lax.axis_size("tx") - 1
    end_y = lax.axis_index("ty") == lax.axis_size("ty") - 1
    col_x = lax.broadcasted_iota(jnp.int32, (1, 1, width_x), 2)
    row_y = lax.broadcasted_iota(jnp.int32, (1, width_y, 1), 1)
    return ((col_x == width_x - 1) & end_x, (row_y == width_y - 1) & end_y)


def fields(tile, rim_x, rim_y):
    last_x, last_y = edge_masks(tile.shape[3], tile.shape[4])
    dx = jnp.concatenate([tile[..., 1:], rim_x], -1) - tile
    dx = jnp.where(last_x, 0.0, dx)
    dy = jnp.concatenate([tile[..., 1:, :], rim_y], -2) - tile
    dy = jnp.where(last_y, 0.0, dy)
    dz = jnp.concatenate(
        [tile[..., 1:, :, :] - tile[..., :-1, :, :], jnp.zeros_like(tile[..., :1, :, :])], -3
    )
    grads = jnp.stack([dx[:, 0], dy[:, 0], dz[:, 0]], 1)
    dirs = jnp.stack([dx[:, 1], dy[:, 1], dz[:, 1]], 1)
    return (grads, dirs)


def moments(grads, dirs, weights):
    wts = weights[:, None, None, None]
    rows = [jnp.sum(wts * grads[:, i] * grads[:, j], 0) for i, j in SYM_PAIRS]
    for i in range(3):
        for j in range(3):
            rows.append(jnp.sum(wts * dirs[:, i] * grads[:, j], 0))
    return jnp.stack(rows, 0)


def couple(moms, grad_own, dir_own):
    trace_m = moms[0] + moms[1] + moms[2]
    mat = [[moms[0], moms[3], moms[4]], [moms[3], moms[1], moms[5]], [moms[4], moms[5], moms[2]]]
    nat = [[moms[6 + 3 * i + j] for j in range(3)] for i in range(3)]
    trace_n = nat[0][0] + nat[1][1] + nat[2][2]
    g_parts = [grad_own[..., i, :, :, :] for i in range(3)]
    e_parts = [dir_own[..., i, :, :, :] for i in range(3)]
    cross_q = []
    cross_p = []
    for i in range(3):
        mg = mat[i][0] * g_parts[0] + mat[i][1] * g_parts[1] + mat[i][2] * g_parts[2]
        me = mat[i][0] * e_parts[0] + mat[i][1] * e_parts[1] + mat[i][2] * e_parts[2]
        ng = nat[i][0] * g_parts[0] + nat[i][1] * g_parts[1] + nat[i][2] * g_parts[2]
        cross_q.append(trace_m * g_parts[i] - mg)
        cross_p.append(trace_m * e_parts[i] - me + trace_n * g_parts[i] - ng)
    return (jnp.stack(cross_q, axis=-4), jnp.stack(cross_p, axis=-4))


def flux_of(tile, rim_x, rim_y, alpha, beta, weights):
    grads, dirs = fields(tile, rim_x, rim_y)
    moms = moments(grads, dirs, weights)
    grad_own = grads[0]
    dir_own = dirs[0]
    cross_q, cross_p = couple(moms, grad_own, dir_own)
    size = jnp.sqrt(jnp.sum(grad_own * grad_own, 0) + EPS_SQ)[None]
    return jnp.stack(
        [beta * grad_own / size + alpha * cross_q, beta * dir_own / size + alpha * cross_p], 0
    )


def model_split(every, rim_x, rim_y, alpha, beta, weights):
    edge_x = flux_of(every[..., -1:], rim_x, rim_y[..., -1:], alpha, beta, weights)[:, 0]
    edge_y = flux_of(every[..., -1:, :], rim_x[..., -1:, :], rim_y, alpha, beta, weights)[:, 1]
    prev_x = passed_dense(edge_x, "tx", 1)
    prev_y = passed_along(edge_y, "ty", 1)
    flux = flux_of(every, rim_x, rim_y, alpha, beta, weights)
    last_x, last_y = edge_masks(flux.shape[3], flux.shape[4])
    flux_x = jnp.where(last_x, 0.0, flux[:, 0])
    flux_y = jnp.where(last_y, 0.0, flux[:, 1])
    flux_z = flux[:, 2]
    flux_z = jnp.concatenate([flux_z[..., :-1, :, :], jnp.zeros_like(flux_z[..., :1, :, :])], -3)
    result = jnp.concatenate([prev_x, flux_x[..., :-1]], -1) - flux_x
    result = result + jnp.concatenate([prev_y, flux_y[..., :-1, :]], -2) - flux_y
    result = (
        result
        + jnp.concatenate([jnp.zeros_like(flux_z[..., :1, :, :]), flux_z[..., :-1, :, :]], -3)
        - flux_z
    )
    return (result[0][None], result[1][None])


def shards(models, direction, coupling, tv_weight):
    mp = lax.axis_size("mp")
    member = lax.axis_index("mp")
    local = models.shape[0]
    own_weights = lax.dynamic_slice_in_dim(coupling, member * local, local)
    alpha = own_weights[0]
    beta = lax.dynamic_slice_in_dim(tv_weight, member * local, local)[0]
    own = jnp.stack([models, direction], 1)
    tiles, weights = [own], [own_weights]
    for shift in range(1, mp):
        tiles.append(lax.ppermute(own, "mp", [(m, (m + shift) % mp) for m in range(mp)]))
        source = (member - shift) % mp
        weights.append(lax.dynamic_slice_in_dim(coupling, source * local, local))
    every = jnp.concatenate(tiles, 0)
    rim_x = passed_dense(every[..., :1], "tx", -1)
    rim_y = passed_along(every[..., :1, :], "ty", -1)
    return model_split(every, rim_x, rim_y, alpha, beta, jnp.concatenate(weights, 0))


def solution(mesh):
    placed = (P("mp", None, "ty", "tx"), P("mp", None, "ty", "tx"), P(), P())
    return jax.shard_map(
        shards,
        mesh=mesh,
        in_specs=placed,
        out_specs=(P("mp", None, "ty", "tx"), P("mp", None, "ty", "tx")),
        check_vma=False,
    )
```

```python
import jax
import jax.numpy as jnp
from jax import lax
from jax.sharding import PartitionSpec as P

EPS_SQ = 0.25
SYM_PAIRS = ((0, 0), (1, 1), (2, 2), (0, 1), (0, 2), (1, 2))


def passed_along(array, axis, by):
    size = lax.axis_size(axis)
    pairs = [(i, i + by) for i in range(size) if 0 <= i + by < size]
    return lax.ppermute(array, axis, pairs)


def passed_dense(array, axis, by):
    count = array.size
    rows = array.reshape(count // 128, 128) if count % 128 == 0 else array.reshape(count)
    return passed_along(rows, axis, by).reshape(array.shape)


def edge_masks(width_y, width_x):
    end_x = lax.axis_index("tx") == lax.axis_size("tx") - 1
    end_y = lax.axis_index("ty") == lax.axis_size("ty") - 1
    col_x = lax.broadcasted_iota(jnp.int32, (1, 1, width_x), 2)
    row_y = lax.broadcasted_iota(jnp.int32, (1, width_y, 1), 1)
    return ((col_x == width_x - 1) & end_x, (row_y == width_y - 1) & end_y)


def fields(tile, rim_x, rim_y):
    last_x, last_y = edge_masks(tile.shape[3], tile.shape[4])
    dx = jnp.concatenate([tile[..., 1:], rim_x], -1) - tile
    dx = jnp.where(last_x, 0.0, dx)
    dy = jnp.concatenate([tile[..., 1:, :], rim_y], -2) - tile
    dy = jnp.where(last_y, 0.0, dy)
    dz = jnp.concatenate(
        [tile[..., 1:, :, :] - tile[..., :-1, :, :], jnp.zeros_like(tile[..., :1, :, :])], -3
    )
    grads = jnp.stack([dx[:, 0], dy[:, 0], dz[:, 0]], 1)
    dirs = jnp.stack([dx[:, 1], dy[:, 1], dz[:, 1]], 1)
    return (grads, dirs)


def moments(grads, dirs, weights):
    wts = weights[:, None, None, None]
    rows = [jnp.sum(wts * grads[:, i] * grads[:, j], 0) for i, j in SYM_PAIRS]
    for i in range(3):
        for j in range(3):
            rows.append(jnp.sum(wts * dirs[:, i] * grads[:, j], 0))
    return jnp.stack(rows, 0)


def couple(moms, grad_own, dir_own):
    trace_m = moms[0] + moms[1] + moms[2]
    mat = [[moms[0], moms[3], moms[4]], [moms[3], moms[1], moms[5]], [moms[4], moms[5], moms[2]]]
    nat = [[moms[6 + 3 * i + j] for j in range(3)] for i in range(3)]
    trace_n = nat[0][0] + nat[1][1] + nat[2][2]
    g_parts = [grad_own[..., i, :, :, :] for i in range(3)]
    e_parts = [dir_own[..., i, :, :, :] for i in range(3)]
    cross_q = []
    cross_p = []
    for i in range(3):
        mg = mat[i][0] * g_parts[0] + mat[i][1] * g_parts[1] + mat[i][2] * g_parts[2]
        me = mat[i][0] * e_parts[0] + mat[i][1] * e_parts[1] + mat[i][2] * e_parts[2]
        ng = nat[i][0] * g_parts[0] + nat[i][1] * g_parts[1] + nat[i][2] * g_parts[2]
        cross_q.append(trace_m * g_parts[i] - mg)
        cross_p.append(trace_m * e_parts[i] - me + trace_n * g_parts[i] - ng)
    return (jnp.stack(cross_q, axis=-4), jnp.stack(cross_p, axis=-4))


def model_split(every, rim_x, rim_y, alpha, beta, weights):
    grads, dirs = fields(every, rim_x, rim_y)
    moms = moments(grads, dirs, weights)
    grad_own = grads[0]
    dir_own = dirs[0]
    cross_q, cross_p = couple(moms, grad_own, dir_own)
    size = jnp.sqrt(jnp.sum(grad_own * grad_own, 0) + EPS_SQ)[None]
    flux = jnp.stack(
        [beta * grad_own / size + alpha * cross_q, beta * dir_own / size + alpha * cross_p], 0
    )
    last_x, last_y = edge_masks(flux.shape[3], flux.shape[4])
    flux_x = jnp.where(last_x, 0.0, flux[:, 0])
    flux_y = jnp.where(last_y, 0.0, flux[:, 1])
    flux_z = flux[:, 2]
    flux_z = jnp.concatenate([flux_z[..., :-1, :, :], jnp.zeros_like(flux_z[..., :1, :, :])], -3)
    prev_x = passed_dense(flux_x[..., -1:], "tx", 1)
    prev_y = passed_along(flux_y[..., -1:, :], "ty", 1)
    result = jnp.concatenate([prev_x, flux_x[..., :-1]], -1) - flux_x
    result = result + jnp.concatenate([prev_y, flux_y[..., :-1, :]], -2) - flux_y
    result = (
        result
        + jnp.concatenate([jnp.zeros_like(flux_z[..., :1, :, :]), flux_z[..., :-1, :, :]], -3)
        - flux_z
    )
    return (result[0][None], result[1][None])


def rim_from(array, axis, shift):
    count = array.size
    rows = array.reshape(count // 128, 128) if count % 128 == 0 else array.reshape(count)
    if shift == 0:
        return passed_along(rows, axis, -1).reshape(array.shape)
    mp = lax.axis_size("mp")
    size = lax.axis_size(axis)
    pairs = [
        (m * size + t, ((m + shift) % mp) * size + t - 1)
        for m in range(mp)
        for t in range(1, size)
    ]
    return lax.ppermute(rows, ("mp", axis), pairs).reshape(array.shape)


def shards(models, direction, coupling, tv_weight):
    mp = lax.axis_size("mp")
    member = lax.axis_index("mp")
    local = models.shape[0]
    own_weights = lax.dynamic_slice_in_dim(coupling, member * local, local)
    alpha = own_weights[0]
    beta = lax.dynamic_slice_in_dim(tv_weight, member * local, local)[0]
    own = jnp.stack([models, direction], 1)
    tiles, rims_x, rims_y, weights = [], [], [], []
    for shift in range(mp):
        if shift == 0:
            tiles.append(own)
        else:
            tiles.append(lax.ppermute(own, "mp", [(m, (m + shift) % mp) for m in range(mp)]))
        rims_x.append(rim_from(own[..., :1], "tx", shift))
        rims_y.append(rim_from(own[..., :1, :], "ty", shift))
        source = (member - shift) % mp
        weights.append(lax.dynamic_slice_in_dim(coupling, source * local, local))
    every = jnp.concatenate(tiles, 0)
    rim_x = jnp.concatenate(rims_x, 0)
    rim_y = jnp.concatenate(rims_y, 0)
    return model_split(every, rim_x, rim_y, alpha, beta, jnp.concatenate(weights, 0))


def solution(mesh):
    placed = (P("mp", None, "ty", "tx"), P("mp", None, "ty", "tx"), P(), P())
    return jax.shard_map(
        shards,
        mesh=mesh,
        in_specs=placed,
        out_specs=(P("mp", None, "ty", "tx"), P("mp", None, "ty", "tx")),
        check_vma=False,
    )
```

```python
import jax
import jax.numpy as jnp
from jax import lax
from jax.sharding import PartitionSpec as P

EPS_SQ = 0.25
SYM_PAIRS = ((0, 0), (1, 1), (2, 2), (0, 1), (0, 2), (1, 2))


def passed_along(array, axis, by):
    size = lax.axis_size(axis)
    pairs = [(i, i + by) for i in range(size) if 0 <= i + by < size]
    return lax.ppermute(array, axis, pairs)


def passed_dense(array, axis, by):
    count = array.size
    rows = array.reshape(count // 128, 128) if count % 128 == 0 else array.reshape(count)
    return passed_along(rows, axis, by).reshape(array.shape)


def edge_masks(width_y, width_x):
    end_x = lax.axis_index("tx") == lax.axis_size("tx") - 1
    end_y = lax.axis_index("ty") == lax.axis_size("ty") - 1
    col_x = lax.broadcasted_iota(jnp.int32, (1, 1, width_x), 2)
    row_y = lax.broadcasted_iota(jnp.int32, (1, width_y, 1), 1)
    return ((col_x == width_x - 1) & end_x, (row_y == width_y - 1) & end_y)


def fields(tile, rim_x, rim_y):
    last_x, last_y = edge_masks(tile.shape[3], tile.shape[4])
    dx = jnp.concatenate([tile[..., 1:], rim_x], -1) - tile
    dx = jnp.where(last_x, 0.0, dx)
    dy = jnp.concatenate([tile[..., 1:, :], rim_y], -2) - tile
    dy = jnp.where(last_y, 0.0, dy)
    dz = jnp.concatenate(
        [tile[..., 1:, :, :] - tile[..., :-1, :, :], jnp.zeros_like(tile[..., :1, :, :])], -3
    )
    grads = jnp.stack([dx[:, 0], dy[:, 0], dz[:, 0]], 1)
    dirs = jnp.stack([dx[:, 1], dy[:, 1], dz[:, 1]], 1)
    return (grads, dirs)


def moments(grads, dirs, weights):
    wts = weights[:, None, None, None]
    rows = [jnp.sum(wts * grads[:, i] * grads[:, j], 0) for i, j in SYM_PAIRS]
    for i in range(3):
        for j in range(3):
            rows.append(jnp.sum(wts * dirs[:, i] * grads[:, j], 0))
    return jnp.stack(rows, 0)


def couple(moms, grad_own, dir_own):
    trace_m = moms[0] + moms[1] + moms[2]
    mat = [[moms[0], moms[3], moms[4]], [moms[3], moms[1], moms[5]], [moms[4], moms[5], moms[2]]]
    nat = [[moms[6 + 3 * i + j] for j in range(3)] for i in range(3)]
    trace_n = nat[0][0] + nat[1][1] + nat[2][2]
    g_parts = [grad_own[..., i, :, :, :] for i in range(3)]
    e_parts = [dir_own[..., i, :, :, :] for i in range(3)]
    cross_q = []
    cross_p = []
    for i in range(3):
        mg = mat[i][0] * g_parts[0] + mat[i][1] * g_parts[1] + mat[i][2] * g_parts[2]
        me = mat[i][0] * e_parts[0] + mat[i][1] * e_parts[1] + mat[i][2] * e_parts[2]
        ng = nat[i][0] * g_parts[0] + nat[i][1] * g_parts[1] + nat[i][2] * g_parts[2]
        cross_q.append(trace_m * g_parts[i] - mg)
        cross_p.append(trace_m * e_parts[i] - me + trace_n * g_parts[i] - ng)
    return (jnp.stack(cross_q, axis=-4), jnp.stack(cross_p, axis=-4))


def diffs(field, rim_x, rim_y, last):
    last_x, last_y = last
    dx = jnp.where(last_x, 0.0, jnp.concatenate([field[..., 1:], rim_x], -1) - field)
    dy = jnp.where(last_y, 0.0, jnp.concatenate([field[:, 1:, :], rim_y], -2) - field)
    dz = jnp.concatenate([field[1:], field[-1:]], 0) - field
    return (dx, dy, dz)


def adjoint_of(flux, prev_x, prev_y, masks):
    last_x, last_y, last_z, first_z = masks
    fx = jnp.where(last_x, 0.0, flux[0])
    fy = jnp.where(last_y, 0.0, flux[1])
    fz = jnp.where(last_z, 0.0, flux[2])
    res = jnp.concatenate([prev_x, fx[..., :-1]], -1) - fx
    res = res + jnp.concatenate([prev_y, fy[:, :-1, :]], -2) - fy
    below = jnp.where(first_z, 0.0, jnp.concatenate([fz[:1], fz[:-1]], 0))
    return res + below - fz


def model_split(every, rim_x, rim_y, alpha, beta, weights):
    depth, width_y, width_x = every.shape[2:]
    end_x = lax.axis_index("tx") == lax.axis_size("tx") - 1
    end_y = lax.axis_index("ty") == lax.axis_size("ty") - 1
    shape = (depth, width_y, width_x)
    col_x = lax.broadcasted_iota(jnp.int32, shape, 2)
    row_y = lax.broadcasted_iota(jnp.int32, shape, 1)
    lev_z = lax.broadcasted_iota(jnp.int32, shape, 0)
    last_x = (col_x == width_x - 1) & end_x
    last_y = (row_y == width_y - 1) & end_y
    last_z = lev_z == depth - 1
    first_z = lev_z == 0
    gs, es = [], []
    for k in range(every.shape[0]):
        gs.append(diffs(every[k, 0], rim_x[k, 0], rim_y[k, 0], (last_x, last_y)))
        es.append(diffs(every[k, 1], rim_x[k, 1], rim_y[k, 1], (last_x, last_y)))

    def summed(terms):
        total = terms[0]
        for term in terms[1:]:
            total = total + term
        return total

    count = len(gs)
    mom = {}
    for i, j in SYM_PAIRS:
        mom[i, j] = summed([weights[k] * gs[k][i] * gs[k][j] for k in range(count)])
        mom[j, i] = mom[i, j]
    nat = {}
    for i in range(3):
        for j in range(3):
            nat[i, j] = summed([weights[k] * es[k][i] * gs[k][j] for k in range(count)])
    trace_m = mom[0, 0] + mom[1, 1] + mom[2, 2]
    trace_n = nat[0, 0] + nat[1, 1] + nat[2, 2]
    g, e = gs[0], es[0]
    size = jnp.sqrt(g[0] * g[0] + g[1] * g[1] + g[2] * g[2] + EPS_SQ)
    flux_q, flux_p = [], []
    for i in range(3):
        mg = mom[i, 0] * g[0] + mom[i, 1] * g[1] + mom[i, 2] * g[2]
        me = mom[i, 0] * e[0] + mom[i, 1] * e[1] + mom[i, 2] * e[2]
        ng = nat[i, 0] * g[0] + nat[i, 1] * g[1] + nat[i, 2] * g[2]
        cross_q = trace_m * g[i] - mg
        cross_p = trace_m * e[i] - me + trace_n * g[i] - ng
        flux_q.append(beta * g[i] / size + alpha * cross_q)
        flux_p.append(beta * e[i] / size + alpha * cross_p)
    edge_x = jnp.stack([flux_q[0][..., -1:], flux_p[0][..., -1:]], 0)
    edge_y = jnp.stack([flux_q[1][:, -1:, :], flux_p[1][:, -1:, :]], 0)
    prev_x = passed_dense(edge_x, "tx", 1)
    prev_y = passed_along(edge_y, "ty", 1)
    masks = (last_x, last_y, last_z, first_z)
    gradient = adjoint_of(flux_q, prev_x[0], prev_y[0], masks)
    hessian = adjoint_of(flux_p, prev_x[1], prev_y[1], masks)
    return (gradient[None], hessian[None])


def shards(models, direction, coupling, tv_weight):
    mp = lax.axis_size("mp")
    member = lax.axis_index("mp")
    local = models.shape[0]
    own_weights = lax.dynamic_slice_in_dim(coupling, member * local, local)
    alpha = own_weights[0]
    beta = lax.dynamic_slice_in_dim(tv_weight, member * local, local)[0]
    own = jnp.stack([models, direction], 1)
    tiles, weights = [own], [own_weights]
    for shift in range(1, mp):
        tiles.append(lax.ppermute(own, "mp", [(m, (m + shift) % mp) for m in range(mp)]))
        source = (member - shift) % mp
        weights.append(lax.dynamic_slice_in_dim(coupling, source * local, local))
    every = jnp.concatenate(tiles, 0)
    rim_x = passed_dense(every[..., :1], "tx", -1)
    rim_y = passed_along(every[..., :1, :], "ty", -1)
    return model_split(every, rim_x, rim_y, alpha, beta, jnp.concatenate(weights, 0))


def solution(mesh):
    placed = (P("mp", None, "ty", "tx"), P("mp", None, "ty", "tx"), P(), P())
    return jax.shard_map(
        shards,
        mesh=mesh,
        in_specs=placed,
        out_specs=(P("mp", None, "ty", "tx"), P("mp", None, "ty", "tx")),
        check_vma=False,
    )
```

```python
import jax
import jax.numpy as jnp
from jax import lax
from jax.sharding import PartitionSpec as P

EPS_SQ = 0.25
SYM_PAIRS = ((0, 0), (1, 1), (2, 2), (0, 1), (0, 2), (1, 2))


def passed_along(array, axis, by):
    size = lax.axis_size(axis)
    pairs = [(i, i + by) for i in range(size) if 0 <= i + by < size]
    return lax.ppermute(array, axis, pairs)


def passed_dense(array, axis, by):
    count = array.size
    rows = array.reshape(count // 128, 128) if count % 128 == 0 else array.reshape(count)
    return passed_along(rows, axis, by).reshape(array.shape)


def edge_masks(width_y, width_x):
    end_x = lax.axis_index("tx") == lax.axis_size("tx") - 1
    end_y = lax.axis_index("ty") == lax.axis_size("ty") - 1
    col_x = lax.broadcasted_iota(jnp.int32, (1, 1, width_x), 2)
    row_y = lax.broadcasted_iota(jnp.int32, (1, width_y, 1), 1)
    return ((col_x == width_x - 1) & end_x, (row_y == width_y - 1) & end_y)


def fields(tile, rim_x, rim_y):
    last_x, last_y = edge_masks(tile.shape[3], tile.shape[4])
    dx = jnp.concatenate([tile[..., 1:], rim_x], -1) - tile
    dx = jnp.where(last_x, 0.0, dx)
    dy = jnp.concatenate([tile[..., 1:, :], rim_y], -2) - tile
    dy = jnp.where(last_y, 0.0, dy)
    dz = jnp.concatenate(
        [tile[..., 1:, :, :] - tile[..., :-1, :, :], jnp.zeros_like(tile[..., :1, :, :])], -3
    )
    grads = jnp.stack([dx[:, 0], dy[:, 0], dz[:, 0]], 1)
    dirs = jnp.stack([dx[:, 1], dy[:, 1], dz[:, 1]], 1)
    return (grads, dirs)


def moments(grads, dirs, weights):
    wts = weights[:, None, None, None]
    rows = [jnp.sum(wts * grads[:, i] * grads[:, j], 0) for i, j in SYM_PAIRS]
    for i in range(3):
        for j in range(3):
            rows.append(jnp.sum(wts * dirs[:, i] * grads[:, j], 0))
    return jnp.stack(rows, 0)


def couple(moms, grad_own, dir_own):
    trace_m = moms[0] + moms[1] + moms[2]
    mat = [[moms[0], moms[3], moms[4]], [moms[3], moms[1], moms[5]], [moms[4], moms[5], moms[2]]]
    nat = [[moms[6 + 3 * i + j] for j in range(3)] for i in range(3)]
    trace_n = nat[0][0] + nat[1][1] + nat[2][2]
    g_parts = [grad_own[..., i, :, :, :] for i in range(3)]
    e_parts = [dir_own[..., i, :, :, :] for i in range(3)]
    cross_q = []
    cross_p = []
    for i in range(3):
        mg = mat[i][0] * g_parts[0] + mat[i][1] * g_parts[1] + mat[i][2] * g_parts[2]
        me = mat[i][0] * e_parts[0] + mat[i][1] * e_parts[1] + mat[i][2] * e_parts[2]
        ng = nat[i][0] * g_parts[0] + nat[i][1] * g_parts[1] + nat[i][2] * g_parts[2]
        cross_q.append(trace_m * g_parts[i] - mg)
        cross_p.append(trace_m * e_parts[i] - me + trace_n * g_parts[i] - ng)
    return (jnp.stack(cross_q, axis=-4), jnp.stack(cross_p, axis=-4))


def model_split(every, rim_x, rim_y, alpha, beta, weights):
    grads, dirs = fields(every, rim_x, rim_y)
    moms = moments(grads, dirs, weights)
    grad_own = grads[0]
    dir_own = dirs[0]
    cross_q, cross_p = couple(moms, grad_own, dir_own)
    size = jnp.sqrt(jnp.sum(grad_own * grad_own, 0) + EPS_SQ)[None]
    flux = jnp.stack(
        [beta * grad_own / size + alpha * cross_q, beta * dir_own / size + alpha * cross_p], 0
    )
    last_x, last_y = edge_masks(flux.shape[3], flux.shape[4])
    flux_x = jnp.where(last_x, 0.0, flux[:, 0])
    flux_y = jnp.where(last_y, 0.0, flux[:, 1])
    levels = lax.broadcasted_iota(jnp.int32, (flux.shape[2], 1, 1), 0)
    flux_z = jnp.where(levels == flux.shape[2] - 1, 0.0, flux[:, 2])
    prev_x = passed_dense(flux_x[..., -1:], "tx", 1)
    prev_y = passed_along(flux_y[..., -1:, :], "ty", 1)

    def adjoint_one(out):
        fx, fy, fz = flux_x[out], flux_y[out], flux_z[out]
        res = jnp.concatenate([prev_x[out], fx[..., :-1]], -1) - fx
        res = res + jnp.concatenate([prev_y[out], fy[..., :-1, :]], -2) - fy
        below = jnp.where(levels == 0, 0.0, jnp.concatenate([fz[:1], fz[:-1]], 0))
        return (res + below - fz)[None]

    return (adjoint_one(0), adjoint_one(1))


def shards(models, direction, coupling, tv_weight):
    mp = lax.axis_size("mp")
    member = lax.axis_index("mp")
    local = models.shape[0]
    own_weights = lax.dynamic_slice_in_dim(coupling, member * local, local)
    alpha = own_weights[0]
    beta = lax.dynamic_slice_in_dim(tv_weight, member * local, local)[0]
    own = jnp.stack([models, direction], 1)
    tiles, weights = [own], [own_weights]
    for shift in range(1, mp):
        tiles.append(lax.ppermute(own, "mp", [(m, (m + shift) % mp) for m in range(mp)]))
        source = (member - shift) % mp
        weights.append(lax.dynamic_slice_in_dim(coupling, source * local, local))
    every = jnp.concatenate(tiles, 0)
    rim_x = passed_dense(every[..., :1], "tx", -1)
    rim_y = passed_along(every[..., :1, :], "ty", -1)
    return model_split(every, rim_x, rim_y, alpha, beta, jnp.concatenate(weights, 0))


def solution(mesh):
    placed = (P("mp", None, "ty", "tx"), P("mp", None, "ty", "tx"), P(), P())
    return jax.shard_map(
        shards,
        mesh=mesh,
        in_specs=placed,
        out_specs=(P("mp", None, "ty", "tx"), P("mp", None, "ty", "tx")),
        check_vma=False,
    )
```

```python
import jax
import jax.numpy as jnp
from jax import lax
from jax.sharding import PartitionSpec as P

EPS_SQ = 0.25
SYM_PAIRS = ((0, 0), (1, 1), (2, 2), (0, 1), (0, 2), (1, 2))


def passed_along(array, axis, by):
    size = lax.axis_size(axis)
    pairs = [(i, i + by) for i in range(size) if 0 <= i + by < size]
    return lax.ppermute(array, axis, pairs)


def passed_dense(array, axis, by):
    count = array.size
    rows = array.reshape(count // 128, 128) if count % 128 == 0 else array.reshape(count)
    return passed_along(rows, axis, by).reshape(array.shape)


def edge_masks(width_y, width_x):
    end_x = lax.axis_index("tx") == lax.axis_size("tx") - 1
    end_y = lax.axis_index("ty") == lax.axis_size("ty") - 1
    col_x = lax.broadcasted_iota(jnp.int32, (1, 1, width_x), 2)
    row_y = lax.broadcasted_iota(jnp.int32, (1, width_y, 1), 1)
    return ((col_x == width_x - 1) & end_x, (row_y == width_y - 1) & end_y)


def fields(tile, rim_x, rim_y):
    last_x, last_y = edge_masks(tile.shape[3], tile.shape[4])
    dx = jnp.concatenate([tile[..., 1:], rim_x], -1) - tile
    dx = jnp.where(last_x, 0.0, dx)
    dy = jnp.concatenate([tile[..., 1:, :], rim_y], -2) - tile
    dy = jnp.where(last_y, 0.0, dy)
    dz = jnp.concatenate(
        [tile[..., 1:, :, :] - tile[..., :-1, :, :], jnp.zeros_like(tile[..., :1, :, :])], -3
    )
    grads = jnp.stack([dx[:, 0], dy[:, 0], dz[:, 0]], 1)
    dirs = jnp.stack([dx[:, 1], dy[:, 1], dz[:, 1]], 1)
    return (grads, dirs)


def moments(grads, dirs, weights):
    wts = weights[:, None, None, None]
    rows = [jnp.sum(wts * grads[:, i] * grads[:, j], 0) for i, j in SYM_PAIRS]
    for i in range(3):
        for j in range(3):
            rows.append(jnp.sum(wts * dirs[:, i] * grads[:, j], 0))
    return rows


def couple(moms, grad_own, dir_own):
    trace_m = moms[0] + moms[1] + moms[2]
    mat = [[moms[0], moms[3], moms[4]], [moms[3], moms[1], moms[5]], [moms[4], moms[5], moms[2]]]
    nat = [[moms[6 + 3 * i + j] for j in range(3)] for i in range(3)]
    trace_n = nat[0][0] + nat[1][1] + nat[2][2]
    g_parts = [grad_own[..., i, :, :, :] for i in range(3)]
    e_parts = [dir_own[..., i, :, :, :] for i in range(3)]
    cross_q = []
    cross_p = []
    for i in range(3):
        mg = mat[i][0] * g_parts[0] + mat[i][1] * g_parts[1] + mat[i][2] * g_parts[2]
        me = mat[i][0] * e_parts[0] + mat[i][1] * e_parts[1] + mat[i][2] * e_parts[2]
        ng = nat[i][0] * g_parts[0] + nat[i][1] * g_parts[1] + nat[i][2] * g_parts[2]
        cross_q.append(trace_m * g_parts[i] - mg)
        cross_p.append(trace_m * e_parts[i] - me + trace_n * g_parts[i] - ng)
    return (jnp.stack(cross_q, axis=-4), jnp.stack(cross_p, axis=-4))


def model_split(own, own_rims, others, other_rims, alpha, beta, own_weights, other_weights):
    own_grads, own_dirs = fields(own, *own_rims)
    own_moms = moments(own_grads, own_dirs, own_weights)
    other_grads, other_dirs = fields(others, *other_rims)
    moms = [a + b for a, b in zip(own_moms, moments(other_grads, other_dirs, other_weights))]
    grad_own = own_grads[0]
    dir_own = own_dirs[0]
    cross_q, cross_p = couple(moms, grad_own, dir_own)
    size = jnp.sqrt(jnp.sum(grad_own * grad_own, 0) + EPS_SQ)[None]
    flux = jnp.stack(
        [beta * grad_own / size + alpha * cross_q, beta * dir_own / size + alpha * cross_p], 0
    )
    last_x, last_y = edge_masks(flux.shape[3], flux.shape[4])
    flux_x = jnp.where(last_x, 0.0, flux[:, 0])
    flux_y = jnp.where(last_y, 0.0, flux[:, 1])
    levels = lax.broadcasted_iota(jnp.int32, (flux.shape[2], 1, 1), 0)
    flux_z = jnp.where(levels == flux.shape[2] - 1, 0.0, flux[:, 2])
    prev_x = passed_dense(flux_x[..., -1:], "tx", 1)
    prev_y = passed_along(flux_y[..., -1:, :], "ty", 1)

    def adjoint_one(out):
        fx, fy, fz = flux_x[out], flux_y[out], flux_z[out]
        res = jnp.concatenate([prev_x[out], fx[..., :-1]], -1) - fx
        res = res + jnp.concatenate([prev_y[out], fy[..., :-1, :]], -2) - fy
        below = jnp.where(levels == 0, 0.0, jnp.concatenate([fz[:1], fz[:-1]], 0))
        return (res + below - fz)[None]

    return (adjoint_one(0), adjoint_one(1))


def shards(models, direction, coupling, tv_weight):
    mp = lax.axis_size("mp")
    member = lax.axis_index("mp")
    local = models.shape[0]
    own_weights = lax.dynamic_slice_in_dim(coupling, member * local, local)
    alpha = own_weights[0]
    beta = lax.dynamic_slice_in_dim(tv_weight, member * local, local)[0]
    own = jnp.stack([models, direction], 1)
    width_y, width_x = own.shape[3], own.shape[4]
    rim_x = passed_dense(own[..., :1], "tx", -1)
    rim_y = passed_along(own[..., :1, :], "ty", -1)
    lanes = jnp.pad(rim_x[..., 0], ((0, 0),) * 3 + ((0, width_x - width_y),))[..., None, :]
    packed = jnp.concatenate([own, rim_y, lanes], -2)
    tiles, weights = [], []
    for shift in range(1, mp):
        tiles.append(lax.ppermute(packed, "mp", [(m, (m + shift) % mp) for m in range(mp)]))
        source = (member - shift) % mp
        weights.append(lax.dynamic_slice_in_dim(coupling, source * local, local))
    every = jnp.concatenate(tiles, 0)
    others = every[..., :width_y, :]
    other_rim_y = every[..., width_y : width_y + 1, :]
    other_rim_x = every[..., width_y + 1, :width_y][..., None]
    return model_split(
        own, (rim_x, rim_y), others, (other_rim_x, other_rim_y),
        alpha, beta, own_weights, jnp.concatenate(weights, 0),
    )


def solution(mesh):
    placed = (P("mp", None, "ty", "tx"), P("mp", None, "ty", "tx"), P(), P())
    return jax.shard_map(
        shards,
        mesh=mesh,
        in_specs=placed,
        out_specs=(P("mp", None, "ty", "tx"), P("mp", None, "ty", "tx")),
        check_vma=False,
    )
```

```python
import jax
import jax.numpy as jnp
from jax import lax
from jax.sharding import PartitionSpec as P

EPS_SQ = 0.25
SYM_PAIRS = ((0, 0), (1, 1), (2, 2), (0, 1), (0, 2), (1, 2))


def passed_along(array, axis, by):
    size = lax.axis_size(axis)
    pairs = [(i, i + by) for i in range(size) if 0 <= i + by < size]
    return lax.ppermute(array, axis, pairs)


def passed_dense(array, axis, by):
    count = array.size
    rows = array.reshape(count // 128, 128) if count % 128 == 0 else array.reshape(count)
    return passed_along(rows, axis, by).reshape(array.shape)


def edge_masks(width_y, width_x):
    end_x = lax.axis_index("tx") == lax.axis_size("tx") - 1
    end_y = lax.axis_index("ty") == lax.axis_size("ty") - 1
    col_x = lax.broadcasted_iota(jnp.int32, (1, 1, width_x), 2)
    row_y = lax.broadcasted_iota(jnp.int32, (1, width_y, 1), 1)
    return ((col_x == width_x - 1) & end_x, (row_y == width_y - 1) & end_y)


def fields(tile, rim_x, rim_y):
    last_x, last_y = edge_masks(tile.shape[3], tile.shape[4])
    dx = jnp.concatenate([tile[..., 1:], rim_x], -1) - tile
    dx = jnp.where(last_x, 0.0, dx)
    dy = jnp.concatenate([tile[..., 1:, :], rim_y], -2) - tile
    dy = jnp.where(last_y, 0.0, dy)
    dz = jnp.concatenate(
        [tile[..., 1:, :, :] - tile[..., :-1, :, :], jnp.zeros_like(tile[..., :1, :, :])], -3
    )
    grads = jnp.stack([dx[:, 0], dy[:, 0], dz[:, 0]], 1)
    dirs = jnp.stack([dx[:, 1], dy[:, 1], dz[:, 1]], 1)
    return (grads, dirs)


def moments(grads, dirs, weights):
    wts = weights[:, None, None, None]
    rows = [jnp.sum(wts * grads[:, i] * grads[:, j], 0) for i, j in SYM_PAIRS]
    for i in range(3):
        for j in range(3):
            rows.append(jnp.sum(wts * dirs[:, i] * grads[:, j], 0))
    return jnp.stack(rows, 0)


def couple(moms, grad_own, dir_own):
    trace_m = moms[0] + moms[1] + moms[2]
    mat = [[moms[0], moms[3], moms[4]], [moms[3], moms[1], moms[5]], [moms[4], moms[5], moms[2]]]
    nat = [[moms[6 + 3 * i + j] for j in range(3)] for i in range(3)]
    trace_n = nat[0][0] + nat[1][1] + nat[2][2]
    g_parts = [grad_own[..., i, :, :, :] for i in range(3)]
    e_parts = [dir_own[..., i, :, :, :] for i in range(3)]
    cross_q = []
    cross_p = []
    for i in range(3):
        mg = mat[i][0] * g_parts[0] + mat[i][1] * g_parts[1] + mat[i][2] * g_parts[2]
        me = mat[i][0] * e_parts[0] + mat[i][1] * e_parts[1] + mat[i][2] * e_parts[2]
        ng = nat[i][0] * g_parts[0] + nat[i][1] * g_parts[1] + nat[i][2] * g_parts[2]
        cross_q.append(trace_m * g_parts[i] - mg)
        cross_p.append(trace_m * e_parts[i] - me + trace_n * g_parts[i] - ng)
    return (jnp.stack(cross_q, axis=-4), jnp.stack(cross_p, axis=-4))


def model_split(every, rim_x, rim_y, alpha, beta, weights):
    grads, dirs = fields(every, rim_x, rim_y)
    moms = moments(grads, dirs, weights)
    grad_own = grads[0]
    dir_own = dirs[0]
    cross_q, cross_p = couple(moms, grad_own, dir_own)
    size = jnp.sqrt(jnp.sum(grad_own * grad_own, 0) + EPS_SQ)[None]
    scale = beta / size
    flux = jnp.stack([grad_own * scale + alpha * cross_q, dir_own * scale + alpha * cross_p], 0)
    last_x, last_y = edge_masks(flux.shape[3], flux.shape[4])
    flux_x = jnp.where(last_x, 0.0, flux[:, 0])
    flux_y = jnp.where(last_y, 0.0, flux[:, 1])
    levels = lax.broadcasted_iota(jnp.int32, (flux.shape[2], 1, 1), 0)
    flux_z = jnp.where(levels == flux.shape[2] - 1, 0.0, flux[:, 2])
    prev_x = passed_dense(flux_x[..., -1:], "tx", 1)
    prev_y = passed_along(flux_y[..., -1:, :], "ty", 1)

    def adjoint_one(out):
        fx, fy, fz = flux_x[out], flux_y[out], flux_z[out]
        res = jnp.concatenate([prev_x[out], fx[..., :-1]], -1) - fx
        res = res + jnp.concatenate([prev_y[out], fy[..., :-1, :]], -2) - fy
        below = jnp.where(levels == 0, 0.0, jnp.concatenate([fz[:1], fz[:-1]], 0))
        return (res + below - fz)[None]

    return (adjoint_one(0), adjoint_one(1))


def shards(models, direction, coupling, tv_weight):
    mp = lax.axis_size("mp")
    member = lax.axis_index("mp")
    local = models.shape[0]
    own_weights = lax.dynamic_slice_in_dim(coupling, member * local, local)
    alpha = own_weights[0]
    beta = lax.dynamic_slice_in_dim(tv_weight, member * local, local)[0]
    own = jnp.stack([models, direction], 1)
    tiles, weights = [own], [own_weights]
    for shift in range(1, mp):
        tiles.append(lax.ppermute(own, "mp", [(m, (m + shift) % mp) for m in range(mp)]))
        source = (member - shift) % mp
        weights.append(lax.dynamic_slice_in_dim(coupling, source * local, local))
    every = jnp.concatenate(tiles, 0)
    rim_x = passed_dense(every[..., :1], "tx", -1)
    rim_y = passed_along(every[..., :1, :], "ty", -1)
    return model_split(every, rim_x, rim_y, alpha, beta, jnp.concatenate(weights, 0))


def solution(mesh):
    placed = (P("mp", None, "ty", "tx"), P("mp", None, "ty", "tx"), P(), P())
    return jax.shard_map(
        shards,
        mesh=mesh,
        in_specs=placed,
        out_specs=(P("mp", None, "ty", "tx"), P("mp", None, "ty", "tx")),
        check_vma=False,
    )
```

```python
import jax
import jax.numpy as jnp
from jax import lax
from jax.sharding import PartitionSpec as P

EPS_SQ = 0.25
SYM_PAIRS = ((0, 0), (1, 1), (2, 2), (0, 1), (0, 2), (1, 2))


def passed_along(array, axis, by):
    size = lax.axis_size(axis)
    pairs = [(i, i + by) for i in range(size) if 0 <= i + by < size]
    return lax.ppermute(array, axis, pairs)


def passed_dense(array, axis, by):
    count = array.size
    rows = array.reshape(count // 128, 128) if count % 128 == 0 else array.reshape(count)
    return passed_along(rows, axis, by).reshape(array.shape)


def edge_masks(width_y, width_x):
    end_x = lax.axis_index("tx") == lax.axis_size("tx") - 1
    end_y = lax.axis_index("ty") == lax.axis_size("ty") - 1
    col_x = lax.broadcasted_iota(jnp.int32, (1, 1, width_x), 2)
    row_y = lax.broadcasted_iota(jnp.int32, (1, width_y, 1), 1)
    return ((col_x == width_x - 1) & end_x, (row_y == width_y - 1) & end_y)


def fields(tile, rim_x, rim_y):
    last_x, last_y = edge_masks(tile.shape[3], tile.shape[4])
    dx = jnp.concatenate([tile[..., 1:], rim_x], -1) - tile
    dx = jnp.where(last_x, 0.0, dx)
    dy = jnp.concatenate([tile[..., 1:, :], rim_y], -2) - tile
    dy = jnp.where(last_y, 0.0, dy)
    dz = jnp.concatenate(
        [tile[..., 1:, :, :] - tile[..., :-1, :, :], jnp.zeros_like(tile[..., :1, :, :])], -3
    )
    grads = jnp.stack([dx[:, 0], dy[:, 0], dz[:, 0]], 1)
    dirs = jnp.stack([dx[:, 1], dy[:, 1], dz[:, 1]], 1)
    return (grads, dirs)


def moments(grads, dirs, weights):
    wts = weights[:, None, None, None]
    rows = [jnp.sum(wts * grads[:, i] * grads[:, j], 0) for i, j in SYM_PAIRS]
    for i in range(3):
        for j in range(3):
            rows.append(jnp.sum(wts * dirs[:, i] * grads[:, j], 0))
    return jnp.stack(rows, 0)


def couple(moms, grad_own, dir_own):
    trace_m = moms[0] + moms[1] + moms[2]
    mat = [[moms[0], moms[3], moms[4]], [moms[3], moms[1], moms[5]], [moms[4], moms[5], moms[2]]]
    nat = [[moms[6 + 3 * i + j] for j in range(3)] for i in range(3)]
    trace_n = nat[0][0] + nat[1][1] + nat[2][2]
    g_parts = [grad_own[..., i, :, :, :] for i in range(3)]
    e_parts = [dir_own[..., i, :, :, :] for i in range(3)]
    cross_q = []
    cross_p = []
    for i in range(3):
        mg = mat[i][0] * g_parts[0] + mat[i][1] * g_parts[1] + mat[i][2] * g_parts[2]
        me = mat[i][0] * e_parts[0] + mat[i][1] * e_parts[1] + mat[i][2] * e_parts[2]
        ng = nat[i][0] * g_parts[0] + nat[i][1] * g_parts[1] + nat[i][2] * g_parts[2]
        cross_q.append(trace_m * g_parts[i] - mg)
        cross_p.append(trace_m * e_parts[i] - me + trace_n * g_parts[i] - ng)
    return (jnp.stack(cross_q, axis=-4), jnp.stack(cross_p, axis=-4))


def model_split(every, rim_x, rim_y, alpha, beta, weights):
    grads, dirs = fields(every, rim_x, rim_y)
    moms = moments(grads, dirs, weights)
    grad_own = grads[0]
    dir_own = dirs[0]
    cross_q, cross_p = couple(moms, grad_own, dir_own)
    size = jnp.sqrt(jnp.sum(grad_own * grad_own, 0) + EPS_SQ)[None]
    flux = jnp.stack(
        [beta * grad_own / size + alpha * cross_q, beta * dir_own / size + alpha * cross_p], 0
    )
    last_x, last_y = edge_masks(flux.shape[3], flux.shape[4])
    flux_x = jnp.where(last_x, 0.0, flux[:, 0])
    flux_y = jnp.where(last_y, 0.0, flux[:, 1])
    levels = lax.broadcasted_iota(jnp.int32, (flux.shape[2], 1, 1), 0)
    flux_z = jnp.where(levels == flux.shape[2] - 1, 0.0, flux[:, 2])
    prev_x = passed_dense(flux_x[..., -1:], "tx", 1)
    prev_y = passed_along(flux_y[..., -1:, :], "ty", 1)

    def adjoint_one(out):
        fx, fy, fz = flux_x[out], flux_y[out], flux_z[out]
        res = jnp.concatenate([prev_x[out], fx[..., :-1]], -1) - fx
        res = res + jnp.concatenate([prev_y[out], fy[..., :-1, :]], -2) - fy
        below = jnp.where(levels == 0, 0.0, jnp.concatenate([fz[:1], fz[:-1]], 0))
        return (res + below - fz)[None]

    return (adjoint_one(0), adjoint_one(1))


def shards(models, direction, coupling, tv_weight):
    mp = lax.axis_size("mp")
    member = lax.axis_index("mp")
    local = models.shape[0]
    own_weights = lax.dynamic_slice_in_dim(coupling, member * local, local)
    alpha = own_weights[0]
    beta = lax.dynamic_slice_in_dim(tv_weight, member * local, local)[0]
    own = jnp.stack([models, direction], 1)
    rim_x = passed_dense(own[..., :1], "tx", -1)
    rim_y = passed_along(own[..., :1, :], "ty", -1)
    rims = jnp.concatenate([rim_x.reshape(-1), rim_y.reshape(-1)])
    rims = rims.reshape(-1, 128) if rims.size % 128 == 0 else rims
    tiles, rims_x, rims_y, weights = [own], [rim_x], [rim_y], [own_weights]
    for shift in range(1, mp):
        pairs = [(m, (m + shift) % mp) for m in range(mp)]
        tiles.append(lax.ppermute(own, "mp", pairs))
        theirs = lax.ppermute(rims, "mp", pairs).reshape(-1)
        rims_x.append(theirs[: rim_x.size].reshape(rim_x.shape))
        rims_y.append(theirs[rim_x.size :].reshape(rim_y.shape))
        source = (member - shift) % mp
        weights.append(lax.dynamic_slice_in_dim(coupling, source * local, local))
    every = jnp.concatenate(tiles, 0)
    rim_x = jnp.concatenate(rims_x, 0)
    rim_y = jnp.concatenate(rims_y, 0)
    return model_split(every, rim_x, rim_y, alpha, beta, jnp.concatenate(weights, 0))


def solution(mesh):
    placed = (P("mp", None, "ty", "tx"), P("mp", None, "ty", "tx"), P(), P())
    return jax.shard_map(
        shards,
        mesh=mesh,
        in_specs=placed,
        out_specs=(P("mp", None, "ty", "tx"), P("mp", None, "ty", "tx")),
        check_vma=False,
    )
```

```python
import jax
import jax.numpy as jnp
from jax import lax
from jax.sharding import PartitionSpec as P
from jax.experimental import pallas as pl
from jax.experimental.pallas import tpu as pltpu

INTERPRET = False

EPS_SQ = 0.25
SYM_PAIRS = ((0, 0), (1, 1), (2, 2), (0, 1), (0, 2), (1, 2))


def passed_along(array, axis, by):
    size = lax.axis_size(axis)
    pairs = [(i, i + by) for i in range(size) if 0 <= i + by < size]
    return lax.ppermute(array, axis, pairs)


def passed_dense(array, axis, by):
    count = array.size
    rows = array.reshape(count // 128, 128) if count % 128 == 0 else array.reshape(count)
    return passed_along(rows, axis, by).reshape(array.shape)


def edge_masks(width_y, width_x):
    end_x = lax.axis_index("tx") == lax.axis_size("tx") - 1
    end_y = lax.axis_index("ty") == lax.axis_size("ty") - 1
    col_x = lax.broadcasted_iota(jnp.int32, (1, 1, width_x), 2)
    row_y = lax.broadcasted_iota(jnp.int32, (1, width_y, 1), 1)
    return ((col_x == width_x - 1) & end_x, (row_y == width_y - 1) & end_y)


def fields(tile, rim_x, rim_y):
    last_x, last_y = edge_masks(tile.shape[3], tile.shape[4])
    dx = jnp.concatenate([tile[..., 1:], rim_x], -1) - tile
    dx = jnp.where(last_x, 0.0, dx)
    dy = jnp.concatenate([tile[..., 1:, :], rim_y], -2) - tile
    dy = jnp.where(last_y, 0.0, dy)
    dz = jnp.concatenate(
        [tile[..., 1:, :, :] - tile[..., :-1, :, :], jnp.zeros_like(tile[..., :1, :, :])], -3
    )
    grads = jnp.stack([dx[:, 0], dy[:, 0], dz[:, 0]], 1)
    dirs = jnp.stack([dx[:, 1], dy[:, 1], dz[:, 1]], 1)
    return (grads, dirs)


def moments(grads, dirs, weights):
    wts = weights[:, None, None, None]
    rows = [jnp.sum(wts * grads[:, i] * grads[:, j], 0) for i, j in SYM_PAIRS]
    for i in range(3):
        for j in range(3):
            rows.append(jnp.sum(wts * dirs[:, i] * grads[:, j], 0))
    return jnp.stack(rows, 0)


def couple(moms, grad_own, dir_own):
    trace_m = moms[0] + moms[1] + moms[2]
    mat = [[moms[0], moms[3], moms[4]], [moms[3], moms[1], moms[5]], [moms[4], moms[5], moms[2]]]
    nat = [[moms[6 + 3 * i + j] for j in range(3)] for i in range(3)]
    trace_n = nat[0][0] + nat[1][1] + nat[2][2]
    g_parts = [grad_own[..., i, :, :, :] for i in range(3)]
    e_parts = [dir_own[..., i, :, :, :] for i in range(3)]
    cross_q = []
    cross_p = []
    for i in range(3):
        mg = mat[i][0] * g_parts[0] + mat[i][1] * g_parts[1] + mat[i][2] * g_parts[2]
        me = mat[i][0] * e_parts[0] + mat[i][1] * e_parts[1] + mat[i][2] * e_parts[2]
        ng = nat[i][0] * g_parts[0] + nat[i][1] * g_parts[1] + nat[i][2] * g_parts[2]
        cross_q.append(trace_m * g_parts[i] - mg)
        cross_p.append(trace_m * e_parts[i] - me + trace_n * g_parts[i] - ng)
    return (jnp.stack(cross_q, axis=-4), jnp.stack(cross_p, axis=-4))


def flux_kernel(scal_ref, flag_ref, ev_ref, rx_ref, ry_ref, pg_ref, ph_ref, ex_ref, ey_ref):
    count, _, depth, width_y, width_x = ev_ref.shape
    lane = lax.broadcasted_iota(jnp.int32, (width_y, width_x), 1)
    row = lax.broadcasted_iota(jnp.int32, (width_y, width_x), 0)
    last_x = (lane == width_x - 1) & (flag_ref[0] == 1)
    last_y = (row == width_y - 1) & (flag_ref[1] == 1)
    alpha = scal_ref[0]
    beta = scal_ref[1]

    def diffs(k, c, z):
        here = ev_ref[k, c, z]
        above = ev_ref[k, c, jnp.minimum(z + 1, depth - 1)]
        next_x = jnp.where(lane == width_x - 1, rx_ref[k, c, z], pltpu.roll(here, width_x - 1, 1))
        next_y = jnp.where(row == width_y - 1, ry_ref[k, c, z], pltpu.roll(here, width_y - 1, 0))
        dx = jnp.where(last_x, 0.0, next_x - here)
        dy = jnp.where(last_y, 0.0, next_y - here)
        return (dx, dy, above - here)

    def adjoint(flux, below, z):
        fx = jnp.where(last_x, 0.0, flux[0])
        fy = jnp.where(last_y, 0.0, flux[1])
        fz = jnp.where(z == depth - 1, 0.0, flux[2])
        res = jnp.where(lane == 0, 0.0, pltpu.roll(fx, 1, 1)) - fx
        res = res + jnp.where(row == 0, 0.0, pltpu.roll(fy, 1, 0)) - fy
        return (res + below - fz, fz)

    def body(z, carry):
        gs = [diffs(k, 0, z) for k in range(count)]
        es = [diffs(k, 1, z) for k in range(count)]
        wts = [scal_ref[2 + k] for k in range(count)]

        def summed(terms):
            total = terms[0]
            for term in terms[1:]:
                total = total + term
            return total

        mom = {}
        for i, j in SYM_PAIRS:
            mom[i, j] = summed([wts[k] * gs[k][i] * gs[k][j] for k in range(count)])
            mom[j, i] = mom[i, j]
        nat = {}
        for i in range(3):
            for j in range(3):
                nat[i, j] = summed([wts[k] * es[k][i] * gs[k][j] for k in range(count)])
        trace_m = mom[0, 0] + mom[1, 1] + mom[2, 2]
        trace_n = nat[0, 0] + nat[1, 1] + nat[2, 2]
        g, e = gs[0], es[0]
        size = jnp.sqrt(g[0] * g[0] + g[1] * g[1] + g[2] * g[2] + EPS_SQ)
        flux_q, flux_p = [], []
        for i in range(3):
            mg = mom[i, 0] * g[0] + mom[i, 1] * g[1] + mom[i, 2] * g[2]
            me = mom[i, 0] * e[0] + mom[i, 1] * e[1] + mom[i, 2] * e[2]
            ng = nat[i, 0] * g[0] + nat[i, 1] * g[1] + nat[i, 2] * g[2]
            cross_q = trace_m * g[i] - mg
            cross_p = trace_m * e[i] - me + trace_n * g[i] - ng
            flux_q.append(beta * g[i] / size + alpha * cross_q)
            flux_p.append(beta * e[i] / size + alpha * cross_p)
        res_g, fz_g = adjoint(flux_q, carry[0], z)
        res_h, fz_h = adjoint(flux_p, carry[1], z)
        pg_ref[z] = res_g
        ph_ref[z] = res_h
        ex_ref[0, z] = flux_q[0][:, width_x - 1 :]
        ex_ref[1, z] = flux_p[0][:, width_x - 1 :]
        ey_ref[0, z] = flux_q[1][width_y - 1 :, :]
        ey_ref[1, z] = flux_p[1][width_y - 1 :, :]
        return (fz_g, fz_h)

    zero = jnp.zeros((width_y, width_x), jnp.float32)
    lax.fori_loop(0, depth, body, (zero, zero))


def model_split(every, rim_x, rim_y, alpha, beta, weights):
    count, _, depth, width_y, width_x = every.shape
    end_x = lax.axis_index("tx") == lax.axis_size("tx") - 1
    end_y = lax.axis_index("ty") == lax.axis_size("ty") - 1
    flags = jnp.stack([end_x, end_y]).astype(jnp.int32)
    scal = jnp.concatenate([jnp.stack([alpha, beta]), weights])
    smem = pl.BlockSpec(memory_space=pltpu.SMEM)
    vmem = pl.BlockSpec(memory_space=pltpu.VMEM)
    tile = jax.ShapeDtypeStruct((depth, width_y, width_x), jnp.float32)
    part_g, part_h, edge_x, edge_y = pl.pallas_call(
        flux_kernel,
        out_shape=(
            tile,
            tile,
            jax.ShapeDtypeStruct((2, depth, width_y, 1), jnp.float32),
            jax.ShapeDtypeStruct((2, depth, 1, width_x), jnp.float32),
        ),
        in_specs=[smem, smem, vmem, vmem, vmem],
        out_specs=(vmem, vmem, vmem, vmem),
        interpret=INTERPRET,
    )(scal, flags, every, rim_x, rim_y)
    prev_x = passed_dense(edge_x, "tx", 1)
    prev_y = passed_along(edge_y, "ty", 1)
    lane = lax.broadcasted_iota(jnp.int32, (1, 1, width_x), 2)
    row = lax.broadcasted_iota(jnp.int32, (1, width_y, 1), 1)
    gradient = part_g + jnp.where(lane == 0, prev_x[0], 0.0) + jnp.where(row == 0, prev_y[0], 0.0)
    hessian = part_h + jnp.where(lane == 0, prev_x[1], 0.0) + jnp.where(row == 0, prev_y[1], 0.0)
    return (gradient[None], hessian[None])


def shards(models, direction, coupling, tv_weight):
    mp = lax.axis_size("mp")
    member = lax.axis_index("mp")
    local = models.shape[0]
    own_weights = lax.dynamic_slice_in_dim(coupling, member * local, local)
    alpha = own_weights[0]
    beta = lax.dynamic_slice_in_dim(tv_weight, member * local, local)[0]
    own = jnp.stack([models, direction], 1)
    rim_x = passed_dense(own[..., :1], "tx", -1)
    rim_y = passed_along(own[..., :1, :], "ty", -1)
    rims = jnp.concatenate([rim_x.reshape(-1), rim_y.reshape(-1)])
    rims = rims.reshape(-1, 128) if rims.size % 128 == 0 else rims
    tiles, rims_x, rims_y, weights = [own], [rim_x], [rim_y], [own_weights]
    for shift in range(1, mp):
        pairs = [(m, (m + shift) % mp) for m in range(mp)]
        tiles.append(lax.ppermute(own, "mp", pairs))
        theirs = lax.ppermute(rims, "mp", pairs).reshape(-1)
        rims_x.append(theirs[: rim_x.size].reshape(rim_x.shape))
        rims_y.append(theirs[rim_x.size :].reshape(rim_y.shape))
        source = (member - shift) % mp
        weights.append(lax.dynamic_slice_in_dim(coupling, source * local, local))
    every = jnp.concatenate(tiles, 0)
    rim_x = jnp.concatenate(rims_x, 0)
    rim_y = jnp.concatenate(rims_y, 0)
    return model_split(every, rim_x, rim_y, alpha, beta, jnp.concatenate(weights, 0))


def solution(mesh):
    placed = (P("mp", None, "ty", "tx"), P("mp", None, "ty", "tx"), P(), P())
    return jax.shard_map(
        shards,
        mesh=mesh,
        in_specs=placed,
        out_specs=(P("mp", None, "ty", "tx"), P("mp", None, "ty", "tx")),
        check_vma=False,
    )
```

```python
import jax
import jax.numpy as jnp
from jax import lax
from jax.sharding import PartitionSpec as P

EPS_SQ = 0.25
SYM_PAIRS = ((0, 0), (1, 1), (2, 2), (0, 1), (0, 2), (1, 2))


def passed_along(array, axis, by):
    size = lax.axis_size(axis)
    pairs = [(i, i + by) for i in range(size) if 0 <= i + by < size]
    return lax.ppermute(array, axis, pairs)


def passed_dense(array, axis, by):
    count = array.size
    rows = array.reshape(count // 128, 128) if count % 128 == 0 else array.reshape(count)
    return passed_along(rows, axis, by).reshape(array.shape)


def edge_masks(width_y, width_x):
    end_x = lax.axis_index("tx") == lax.axis_size("tx") - 1
    end_y = lax.axis_index("ty") == lax.axis_size("ty") - 1
    col_x = lax.broadcasted_iota(jnp.int32, (1, 1, width_x), 2)
    row_y = lax.broadcasted_iota(jnp.int32, (1, width_y, 1), 1)
    return ((col_x == width_x - 1) & end_x, (row_y == width_y - 1) & end_y)


def fields(tile, rim_x, rim_y):
    last_x, last_y = edge_masks(tile.shape[3], tile.shape[4])
    dx = jnp.concatenate([tile[..., 1:], rim_x], -1) - tile
    dx = jnp.where(last_x, 0.0, dx)
    dy = jnp.concatenate([tile[..., 1:, :], rim_y], -2) - tile
    dy = jnp.where(last_y, 0.0, dy)
    dz = jnp.concatenate(
        [tile[..., 1:, :, :] - tile[..., :-1, :, :], jnp.zeros_like(tile[..., :1, :, :])], -3
    )
    grads = jnp.stack([dx[:, 0], dy[:, 0], dz[:, 0]], 1)
    dirs = jnp.stack([dx[:, 1], dy[:, 1], dz[:, 1]], 1)
    return (grads, dirs)


def moments(grads, dirs, weights):
    wts = weights[:, None, None, None]
    rows = [jnp.sum(wts * grads[:, i] * grads[:, j], 0) for i, j in SYM_PAIRS]
    for i in range(3):
        for j in range(3):
            rows.append(jnp.sum(wts * dirs[:, i] * grads[:, j], 0))
    return jnp.stack(rows, 0)


def couple(moms, grad_own, dir_own):
    trace_m = moms[0] + moms[1] + moms[2]
    mat = [[moms[0], moms[3], moms[4]], [moms[3], moms[1], moms[5]], [moms[4], moms[5], moms[2]]]
    nat = [[moms[6 + 3 * i + j] for j in range(3)] for i in range(3)]
    trace_n = nat[0][0] + nat[1][1] + nat[2][2]
    g_parts = [grad_own[..., i, :, :, :] for i in range(3)]
    e_parts = [dir_own[..., i, :, :, :] for i in range(3)]
    cross_q = []
    cross_p = []
    for i in range(3):
        mg = mat[i][0] * g_parts[0] + mat[i][1] * g_parts[1] + mat[i][2] * g_parts[2]
        me = mat[i][0] * e_parts[0] + mat[i][1] * e_parts[1] + mat[i][2] * e_parts[2]
        ng = nat[i][0] * g_parts[0] + nat[i][1] * g_parts[1] + nat[i][2] * g_parts[2]
        cross_q.append(trace_m * g_parts[i] - mg)
        cross_p.append(trace_m * e_parts[i] - me + trace_n * g_parts[i] - ng)
    return (jnp.stack(cross_q, axis=-4), jnp.stack(cross_p, axis=-4))


def model_split(every, rim_x, rim_y, alpha, beta, weights):
    grads, dirs = fields(every, rim_x, rim_y)
    moms = moments(grads, dirs, weights)
    grad_own = grads[0]
    dir_own = dirs[0]
    cross_q, cross_p = couple(moms, grad_own, dir_own)
    size = jnp.sqrt(jnp.sum(grad_own * grad_own, 0) + EPS_SQ)[None]
    flux = jnp.stack(
        [beta * grad_own / size + alpha * cross_q, beta * dir_own / size + alpha * cross_p], 0
    )
    last_x, last_y = edge_masks(flux.shape[3], flux.shape[4])
    flux_x = jnp.where(last_x, 0.0, flux[:, 0])
    flux_y = jnp.where(last_y, 0.0, flux[:, 1])
    levels = lax.broadcasted_iota(jnp.int32, (flux.shape[2], 1, 1), 0)
    flux_z = jnp.where(levels == flux.shape[2] - 1, 0.0, flux[:, 2])
    prev_x = passed_dense(flux_x[..., -1:], "tx", 1)
    prev_y = passed_along(flux_y[..., -1:, :], "ty", 1)

    def adjoint_one(out):
        fx, fy, fz = flux_x[out], flux_y[out], flux_z[out]
        res = jnp.concatenate([prev_x[out], fx[..., :-1]], -1) - fx
        res = res + jnp.concatenate([prev_y[out], fy[..., :-1, :]], -2) - fy
        below = jnp.where(levels == 0, 0.0, jnp.concatenate([fz[:1], fz[:-1]], 0))
        return (res + below - fz)[None]

    return (adjoint_one(0), adjoint_one(1))


def shards(models, direction, coupling, tv_weight):
    mp = lax.axis_size("mp")
    member = lax.axis_index("mp")
    local = models.shape[0]
    own_weights = lax.dynamic_slice_in_dim(coupling, member * local, local)
    alpha = own_weights[0]
    beta = lax.dynamic_slice_in_dim(tv_weight, member * local, local)[0]
    own = jnp.stack([models, direction], 1)
    def fetched(edges):
        return (passed_dense(edges[0], "tx", -1), passed_along(edges[1], "ty", -1))

    def skipped(edges):
        return (jnp.zeros_like(edges[0]), jnp.zeros_like(edges[1]))

    rim_x, rim_y = lax.cond(member >= 0, fetched, skipped, (own[..., :1], own[..., :1, :]))
    rims = jnp.concatenate([rim_x.reshape(-1), rim_y.reshape(-1)])
    rims = rims.reshape(-1, 128) if rims.size % 128 == 0 else rims
    tiles, rims_x, rims_y, weights = [own], [rim_x], [rim_y], [own_weights]
    for shift in range(1, mp):
        pairs = [(m, (m + shift) % mp) for m in range(mp)]
        tiles.append(lax.ppermute(own, "mp", pairs))
        theirs = lax.ppermute(rims, "mp", pairs).reshape(-1)
        rims_x.append(theirs[: rim_x.size].reshape(rim_x.shape))
        rims_y.append(theirs[rim_x.size :].reshape(rim_y.shape))
        source = (member - shift) % mp
        weights.append(lax.dynamic_slice_in_dim(coupling, source * local, local))
    every = jnp.concatenate(tiles, 0)
    rim_x = jnp.concatenate(rims_x, 0)
    rim_y = jnp.concatenate(rims_y, 0)
    return model_split(every, rim_x, rim_y, alpha, beta, jnp.concatenate(weights, 0))


def solution(mesh):
    placed = (P("mp", None, "ty", "tx"), P("mp", None, "ty", "tx"), P(), P())
    return jax.shard_map(
        shards,
        mesh=mesh,
        in_specs=placed,
        out_specs=(P("mp", None, "ty", "tx"), P("mp", None, "ty", "tx")),
        check_vma=False,
    )
```

```python
import jax
import jax.numpy as jnp
from jax import lax
from jax.sharding import PartitionSpec as P

EPS_SQ = 0.25
SYM_PAIRS = ((0, 0), (1, 1), (2, 2), (0, 1), (0, 2), (1, 2))


def passed_along(array, axis, by):
    size = lax.axis_size(axis)
    pairs = [(i, i + by) for i in range(size) if 0 <= i + by < size]
    return lax.ppermute(array, axis, pairs)


def passed_dense(array, axis, by):
    count = array.size
    rows = array.reshape(count // 128, 128) if count % 128 == 0 else array.reshape(count)
    return passed_along(rows, axis, by).reshape(array.shape)


def edge_masks(width_y, width_x):
    end_x = lax.axis_index("tx") == lax.axis_size("tx") - 1
    end_y = lax.axis_index("ty") == lax.axis_size("ty") - 1
    col_x = lax.broadcasted_iota(jnp.int32, (1, 1, width_x), 2)
    row_y = lax.broadcasted_iota(jnp.int32, (1, width_y, 1), 1)
    return ((col_x == width_x - 1) & end_x, (row_y == width_y - 1) & end_y)


def fields(tile, rim_x, rim_y):
    last_x, last_y = edge_masks(tile.shape[3], tile.shape[4])
    dx = jnp.concatenate([tile[..., 1:], rim_x], -1) - tile
    dx = jnp.where(last_x, 0.0, dx)
    dy = jnp.concatenate([tile[..., 1:, :], rim_y], -2) - tile
    dy = jnp.where(last_y, 0.0, dy)
    dz = jnp.concatenate(
        [tile[..., 1:, :, :] - tile[..., :-1, :, :], jnp.zeros_like(tile[..., :1, :, :])], -3
    )
    grads = jnp.stack([dx[:, 0], dy[:, 0], dz[:, 0]], 1)
    dirs = jnp.stack([dx[:, 1], dy[:, 1], dz[:, 1]], 1)
    return (grads, dirs)


def moments(grads, dirs, weights):
    wts = weights[:, None, None, None]
    rows = [jnp.sum(wts * grads[:, i] * grads[:, j], 0) for i, j in SYM_PAIRS]
    for i in range(3):
        for j in range(3):
            rows.append(jnp.sum(wts * dirs[:, i] * grads[:, j], 0))
    return jnp.stack(rows, 0)


def couple(moms, grad_own, dir_own):
    trace_m = moms[0] + moms[1] + moms[2]
    mat = [[moms[0], moms[3], moms[4]], [moms[3], moms[1], moms[5]], [moms[4], moms[5], moms[2]]]
    nat = [[moms[6 + 3 * i + j] for j in range(3)] for i in range(3)]
    trace_n = nat[0][0] + nat[1][1] + nat[2][2]
    g_parts = [grad_own[..., i, :, :, :] for i in range(3)]
    e_parts = [dir_own[..., i, :, :, :] for i in range(3)]
    cross_q = []
    cross_p = []
    for i in range(3):
        mg = mat[i][0] * g_parts[0] + mat[i][1] * g_parts[1] + mat[i][2] * g_parts[2]
        me = mat[i][0] * e_parts[0] + mat[i][1] * e_parts[1] + mat[i][2] * e_parts[2]
        ng = nat[i][0] * g_parts[0] + nat[i][1] * g_parts[1] + nat[i][2] * g_parts[2]
        cross_q.append(trace_m * g_parts[i] - mg)
        cross_p.append(trace_m * e_parts[i] - me + trace_n * g_parts[i] - ng)
    return (jnp.stack(cross_q, axis=-4), jnp.stack(cross_p, axis=-4))


def model_split(every, rim_x, rim_y, alpha, beta, weights):
    grads, dirs = fields(every, rim_x, rim_y)
    moms = moments(grads, dirs, weights)
    grad_own = grads[0]
    dir_own = dirs[0]
    cross_q, cross_p = couple(moms, grad_own, dir_own)
    size = jnp.sqrt(jnp.sum(grad_own * grad_own, 0) + EPS_SQ)[None]
    flux = jnp.stack(
        [beta * grad_own / size + alpha * cross_q, beta * dir_own / size + alpha * cross_p], 0
    )
    last_x, last_y = edge_masks(flux.shape[3], flux.shape[4])
    flux_x = jnp.where(last_x, 0.0, flux[:, 0])
    flux_y = jnp.where(last_y, 0.0, flux[:, 1])
    levels = lax.broadcasted_iota(jnp.int32, (flux.shape[2], 1, 1), 0)
    flux_z = jnp.where(levels == flux.shape[2] - 1, 0.0, flux[:, 2])
    prev_x = passed_dense(flux_x[..., -1:], "tx", 1)
    prev_y = passed_along(flux_y[..., -1:, :], "ty", 1)

    def adjoint_one(out):
        fx, fy, fz = flux_x[out], flux_y[out], flux_z[out]
        res = jnp.concatenate([prev_x[out], fx[..., :-1]], -1) - fx
        res = res + jnp.concatenate([prev_y[out], fy[..., :-1, :]], -2) - fy
        below = jnp.where(levels == 0, 0.0, jnp.concatenate([fz[:1], fz[:-1]], 0))
        return (res + below - fz)[None]

    return (adjoint_one(0), adjoint_one(1))


def shards(models, direction, coupling, tv_weight):
    mp = lax.axis_size("mp")
    member = lax.axis_index("mp")
    local = models.shape[0]
    own_weights = lax.dynamic_slice_in_dim(coupling, member * local, local)
    alpha = own_weights[0]
    beta = lax.dynamic_slice_in_dim(tv_weight, member * local, local)[0]
    own = jnp.stack([models, direction], 1)
    rim_x = passed_dense(own[..., :1], "tx", -1)
    rim_y = passed_along(own[..., :1, :], "ty", -1)
    packed = jnp.concatenate([own.reshape(-1), rim_x.reshape(-1), rim_y.reshape(-1)])
    packed = packed.reshape(-1, 128) if packed.size % 128 == 0 else packed
    tiles, rims_x, rims_y, weights = [own], [rim_x], [rim_y], [own_weights]
    for shift in range(1, mp):
        pairs = [(m, (m + shift) % mp) for m in range(mp)]
        theirs = lax.ppermute(packed, "mp", pairs).reshape(-1)
        cut = own.size + rim_x.size
        tiles.append(theirs[: own.size].reshape(own.shape))
        rims_x.append(theirs[own.size : cut].reshape(rim_x.shape))
        rims_y.append(theirs[cut:].reshape(rim_y.shape))
        source = (member - shift) % mp
        weights.append(lax.dynamic_slice_in_dim(coupling, source * local, local))
    every = jnp.concatenate(tiles, 0)
    rim_x = jnp.concatenate(rims_x, 0)
    rim_y = jnp.concatenate(rims_y, 0)
    return model_split(every, rim_x, rim_y, alpha, beta, jnp.concatenate(weights, 0))


def solution(mesh):
    placed = (P("mp", None, "ty", "tx"), P("mp", None, "ty", "tx"), P(), P())
    return jax.shard_map(
        shards,
        mesh=mesh,
        in_specs=placed,
        out_specs=(P("mp", None, "ty", "tx"), P("mp", None, "ty", "tx")),
        check_vma=False,
    )
```

```python
import jax
import jax.numpy as jnp
from jax import lax
from jax.sharding import PartitionSpec as P

EPS_SQ = 0.25
SYM_PAIRS = ((0, 0), (1, 1), (2, 2), (0, 1), (0, 2), (1, 2))


def passed_along(array, axis, by):
    size = lax.axis_size(axis)
    pairs = [(i, i + by) for i in range(size) if 0 <= i + by < size]
    return lax.ppermute(array, axis, pairs)


def passed_dense(array, axis, by):
    count = array.size
    rows = array.reshape(count // 128, 128) if count % 128 == 0 else array.reshape(count)
    return passed_along(rows, axis, by).reshape(array.shape)


def edge_masks(width_y, width_x):
    end_x = lax.axis_index("tx") == lax.axis_size("tx") - 1
    end_y = lax.axis_index("ty") == lax.axis_size("ty") - 1
    col_x = lax.broadcasted_iota(jnp.int32, (1, 1, width_x), 2)
    row_y = lax.broadcasted_iota(jnp.int32, (1, width_y, 1), 1)
    return ((col_x == width_x - 1) & end_x, (row_y == width_y - 1) & end_y)


def fields(tile, rim_x, rim_y):
    last_x, last_y = edge_masks(tile.shape[3], tile.shape[4])
    dx = jnp.concatenate([tile[..., 1:], rim_x], -1) - tile
    dx = jnp.where(last_x, 0.0, dx)
    dy = jnp.concatenate([tile[..., 1:, :], rim_y], -2) - tile
    dy = jnp.where(last_y, 0.0, dy)
    dz = jnp.concatenate(
        [tile[..., 1:, :, :] - tile[..., :-1, :, :], jnp.zeros_like(tile[..., :1, :, :])], -3
    )
    grads = jnp.stack([dx[:, 0], dy[:, 0], dz[:, 0]], 1)
    dirs = jnp.stack([dx[:, 1], dy[:, 1], dz[:, 1]], 1)
    return (grads, dirs)


def moments(grads, dirs, weights):
    wts = weights[:, None, None, None]
    rows = [jnp.sum(wts * grads[:, i] * grads[:, j], 0) for i, j in SYM_PAIRS]
    for i in range(3):
        for j in range(3):
            rows.append(jnp.sum(wts * dirs[:, i] * grads[:, j], 0))
    return jnp.stack(rows, 0)


def couple(moms, grad_own, dir_own):
    trace_m = moms[0] + moms[1] + moms[2]
    mat = [[moms[0], moms[3], moms[4]], [moms[3], moms[1], moms[5]], [moms[4], moms[5], moms[2]]]
    nat = [[moms[6 + 3 * i + j] for j in range(3)] for i in range(3)]
    trace_n = nat[0][0] + nat[1][1] + nat[2][2]
    g_parts = [grad_own[..., i, :, :, :] for i in range(3)]
    e_parts = [dir_own[..., i, :, :, :] for i in range(3)]
    cross_q = []
    cross_p = []
    for i in range(3):
        mg = mat[i][0] * g_parts[0] + mat[i][1] * g_parts[1] + mat[i][2] * g_parts[2]
        me = mat[i][0] * e_parts[0] + mat[i][1] * e_parts[1] + mat[i][2] * e_parts[2]
        ng = nat[i][0] * g_parts[0] + nat[i][1] * g_parts[1] + nat[i][2] * g_parts[2]
        cross_q.append(trace_m * g_parts[i] - mg)
        cross_p.append(trace_m * e_parts[i] - me + trace_n * g_parts[i] - ng)
    return (jnp.stack(cross_q, axis=-4), jnp.stack(cross_p, axis=-4))


def model_split(every, rim_x, rim_y, alpha, beta, weights):
    grads, dirs = fields(every, rim_x, rim_y)
    moms = moments(grads, dirs, weights)
    grad_own = grads[0]
    dir_own = dirs[0]
    cross_q, cross_p = couple(moms, grad_own, dir_own)
    size = jnp.sqrt(jnp.sum(grad_own * grad_own, 0) + EPS_SQ)[None]
    flux = jnp.stack(
        [beta * grad_own / size + alpha * cross_q, beta * dir_own / size + alpha * cross_p], 0
    )
    last_x, last_y = edge_masks(flux.shape[3], flux.shape[4])
    flux_x = jnp.where(last_x, 0.0, flux[:, 0])
    flux_y = jnp.where(last_y, 0.0, flux[:, 1])
    levels = lax.broadcasted_iota(jnp.int32, (flux.shape[2], 1, 1), 0)
    flux_z = jnp.where(levels == flux.shape[2] - 1, 0.0, flux[:, 2])
    prev_x = passed_dense(flux_x[..., -1:], "tx", 1)
    prev_y = passed_along(flux_y[..., -1:, :], "ty", 1)

    def adjoint_one(out):
        fx, fy, fz = flux_x[out], flux_y[out], flux_z[out]
        res = jnp.concatenate([prev_x[out], fx[..., :-1]], -1) - fx
        res = res + jnp.concatenate([prev_y[out], fy[..., :-1, :]], -2) - fy
        below = jnp.where(levels == 0, 0.0, jnp.concatenate([fz[:1], fz[:-1]], 0))
        return (res + below - fz)[None]

    return (adjoint_one(0), adjoint_one(1))


def shards(models, direction, coupling, tv_weight):
    mp = lax.axis_size("mp")
    member = lax.axis_index("mp")
    local = models.shape[0]
    own_weights = lax.dynamic_slice_in_dim(coupling, member * local, local)
    alpha = own_weights[0]
    beta = lax.dynamic_slice_in_dim(tv_weight, member * local, local)[0]
    own = jnp.stack([models, direction], 1)
    rim_x = passed_dense(jnp.stack([models[..., :1], direction[..., :1]], 1), "tx", -1)
    rim_y = passed_along(jnp.stack([models[..., :1, :], direction[..., :1, :]], 1), "ty", -1)
    rims = jnp.concatenate([rim_x.reshape(-1), rim_y.reshape(-1)])
    rims = rims.reshape(-1, 128) if rims.size % 128 == 0 else rims
    tiles, rims_x, rims_y, weights = [own], [rim_x], [rim_y], [own_weights]
    for shift in range(1, mp):
        pairs = [(m, (m + shift) % mp) for m in range(mp)]
        parts = [lax.ppermute(part, "mp", pairs) for part in (models, direction)]
        tiles.append(jnp.stack(parts, 1))
        theirs = lax.ppermute(rims, "mp", pairs).reshape(-1)
        rims_x.append(theirs[: rim_x.size].reshape(rim_x.shape))
        rims_y.append(theirs[rim_x.size :].reshape(rim_y.shape))
        source = (member - shift) % mp
        weights.append(lax.dynamic_slice_in_dim(coupling, source * local, local))
    every = jnp.concatenate(tiles, 0)
    rim_x = jnp.concatenate(rims_x, 0)
    rim_y = jnp.concatenate(rims_y, 0)
    return model_split(every, rim_x, rim_y, alpha, beta, jnp.concatenate(weights, 0))


def solution(mesh):
    placed = (P("mp", None, "ty", "tx"), P("mp", None, "ty", "tx"), P(), P())
    return jax.shard_map(
        shards,
        mesh=mesh,
        in_specs=placed,
        out_specs=(P("mp", None, "ty", "tx"), P("mp", None, "ty", "tx")),
        check_vma=False,
    )
```

```python
import jax
import jax.numpy as jnp
from jax import lax
from jax.sharding import PartitionSpec as P

EPS_SQ = 0.25
SYM_PAIRS = ((0, 0), (1, 1), (2, 2), (0, 1), (0, 2), (1, 2))


def passed_along(array, axis, by):
    size = lax.axis_size(axis)
    pairs = [(i, i + by) for i in range(size) if 0 <= i + by < size]
    return lax.ppermute(array, axis, pairs)


def passed_dense(array, axis, by):
    count = array.size
    rows = array.reshape(count // 128, 128) if count % 128 == 0 else array.reshape(count)
    return passed_along(rows, axis, by).reshape(array.shape)


def edge_masks(width_y, width_x):
    end_x = lax.axis_index("tx") == lax.axis_size("tx") - 1
    end_y = lax.axis_index("ty") == lax.axis_size("ty") - 1
    col_x = lax.broadcasted_iota(jnp.int32, (1, 1, width_x), 2)
    row_y = lax.broadcasted_iota(jnp.int32, (1, width_y, 1), 1)
    return ((col_x == width_x - 1) & end_x, (row_y == width_y - 1) & end_y)


def fields(tile, rim_x, rim_y):
    last_x, last_y = edge_masks(tile.shape[3], tile.shape[4])
    dx = jnp.concatenate([tile[..., 1:], rim_x], -1) - tile
    dx = jnp.where(last_x, 0.0, dx)
    dy = jnp.concatenate([tile[..., 1:, :], rim_y], -2) - tile
    dy = jnp.where(last_y, 0.0, dy)
    dz = jnp.concatenate(
        [tile[..., 1:, :, :] - tile[..., :-1, :, :], jnp.zeros_like(tile[..., :1, :, :])], -3
    )
    grads = jnp.stack([dx[:, 0], dy[:, 0], dz[:, 0]], 1)
    dirs = jnp.stack([dx[:, 1], dy[:, 1], dz[:, 1]], 1)
    return (grads, dirs)


def moments(grads, dirs, weights):
    wts = weights[:, None, None, None]
    rows = [jnp.sum(wts * grads[:, i] * grads[:, j], 0) for i, j in SYM_PAIRS]
    for i in range(3):
        for j in range(3):
            rows.append(jnp.sum(wts * dirs[:, i] * grads[:, j], 0))
    return jnp.stack(rows, 0)


def couple(moms, grad_own, dir_own):
    trace_m = moms[0] + moms[1] + moms[2]
    mat = [[moms[0], moms[3], moms[4]], [moms[3], moms[1], moms[5]], [moms[4], moms[5], moms[2]]]
    nat = [[moms[6 + 3 * i + j] for j in range(3)] for i in range(3)]
    trace_n = nat[0][0] + nat[1][1] + nat[2][2]
    g_parts = [grad_own[..., i, :, :, :] for i in range(3)]
    e_parts = [dir_own[..., i, :, :, :] for i in range(3)]
    cross_q = []
    cross_p = []
    for i in range(3):
        mg = mat[i][0] * g_parts[0] + mat[i][1] * g_parts[1] + mat[i][2] * g_parts[2]
        me = mat[i][0] * e_parts[0] + mat[i][1] * e_parts[1] + mat[i][2] * e_parts[2]
        ng = nat[i][0] * g_parts[0] + nat[i][1] * g_parts[1] + nat[i][2] * g_parts[2]
        cross_q.append(trace_m * g_parts[i] - mg)
        cross_p.append(trace_m * e_parts[i] - me + trace_n * g_parts[i] - ng)
    return (jnp.stack(cross_q, axis=-4), jnp.stack(cross_p, axis=-4))


def model_split(every, rim_x, rim_y, alpha, beta, weights):
    grads, dirs = fields(every, rim_x, rim_y)
    moms = moments(grads, dirs, weights)
    grad_own = grads[0]
    dir_own = dirs[0]
    cross_q, cross_p = couple(moms, grad_own, dir_own)
    size = jnp.sqrt(jnp.sum(grad_own * grad_own, 0) + EPS_SQ)[None]
    flux = jnp.stack(
        [beta * grad_own / size + alpha * cross_q, beta * dir_own / size + alpha * cross_p], 0
    )
    last_x, last_y = edge_masks(flux.shape[3], flux.shape[4])
    flux_x = jnp.where(last_x, 0.0, flux[:, 0])
    flux_y = jnp.where(last_y, 0.0, flux[:, 1])
    levels = lax.broadcasted_iota(jnp.int32, (flux.shape[2], 1, 1), 0)
    flux_z = jnp.where(levels == flux.shape[2] - 1, 0.0, flux[:, 2])
    prev_x = passed_dense(flux_x[..., -1:], "tx", 1)
    prev_y = passed_along(flux_y[..., -1:, :], "ty", 1)

    def adjoint_one(out):
        fx, fy, fz = flux_x[out], flux_y[out], flux_z[out]
        res = jnp.concatenate([prev_x[out], fx[..., :-1]], -1) - fx
        res = res + jnp.concatenate([prev_y[out], fy[..., :-1, :]], -2) - fy
        below = jnp.where(levels == 0, 0.0, jnp.concatenate([fz[:1], fz[:-1]], 0))
        return (res + below - fz)[None]

    return (adjoint_one(0), adjoint_one(1))


def shards(models, direction, coupling, tv_weight):
    mp = lax.axis_size("mp")
    member = lax.axis_index("mp")
    local = models.shape[0]
    order = (member - jnp.arange(mp)) % mp
    picks = (order[:, None] * local + jnp.arange(local)[None, :]).reshape(-1)
    weights = jnp.take(coupling, picks)
    alpha = weights[0]
    beta = jnp.take(tv_weight, picks[:1])[0]
    own = jnp.stack([models, direction], 1)
    rim_x = passed_dense(own[..., :1], "tx", -1)
    rim_y = passed_along(own[..., :1, :], "ty", -1)
    rims = jnp.concatenate([rim_x.reshape(-1), rim_y.reshape(-1)])
    rims = rims.reshape(-1, 128) if rims.size % 128 == 0 else rims
    tiles, rims_x, rims_y = [own], [rim_x], [rim_y]
    for shift in range(1, mp):
        pairs = [(m, (m + shift) % mp) for m in range(mp)]
        tiles.append(lax.ppermute(own, "mp", pairs))
        theirs = lax.ppermute(rims, "mp", pairs).reshape(-1)
        rims_x.append(theirs[: rim_x.size].reshape(rim_x.shape))
        rims_y.append(theirs[rim_x.size :].reshape(rim_y.shape))
    every = jnp.concatenate(tiles, 0)
    rim_x = jnp.concatenate(rims_x, 0)
    rim_y = jnp.concatenate(rims_y, 0)
    return model_split(every, rim_x, rim_y, alpha, beta, weights)


def solution(mesh):
    placed = (P("mp", None, "ty", "tx"), P("mp", None, "ty", "tx"), P(), P())
    return jax.shard_map(
        shards,
        mesh=mesh,
        in_specs=placed,
        out_specs=(P("mp", None, "ty", "tx"), P("mp", None, "ty", "tx")),
        check_vma=False,
    )
```

```python
import jax
import jax.numpy as jnp
from jax import lax
from jax.sharding import PartitionSpec as P

EPS_SQ = 0.25
SYM_PAIRS = ((0, 0), (1, 1), (2, 2), (0, 1), (0, 2), (1, 2))


def passed_along(array, axis, by):
    size = lax.axis_size(axis)
    pairs = [(i, i + by) for i in range(size) if 0 <= i + by < size]
    return lax.ppermute(array, axis, pairs)


def passed_dense(array, axis, by):
    count = array.size
    rows = array.reshape(count // 128, 128) if count % 128 == 0 else array.reshape(count)
    return passed_along(rows, axis, by).reshape(array.shape)


def edge_masks(width_y, width_x):
    end_x = lax.axis_index("tx") == lax.axis_size("tx") - 1
    end_y = lax.axis_index("ty") == lax.axis_size("ty") - 1
    col_x = lax.broadcasted_iota(jnp.int32, (1, 1, width_x), 2)
    row_y = lax.broadcasted_iota(jnp.int32, (1, width_y, 1), 1)
    return ((col_x == width_x - 1) & end_x, (row_y == width_y - 1) & end_y)


def fields(tile, rim_x, rim_y):
    last_x, last_y = edge_masks(tile.shape[3], tile.shape[4])
    dx = jnp.concatenate([tile[..., 1:], rim_x], -1) - tile
    dx = jnp.where(last_x, 0.0, dx)
    dy = jnp.concatenate([tile[..., 1:, :], rim_y], -2) - tile
    dy = jnp.where(last_y, 0.0, dy)
    dz = jnp.concatenate(
        [tile[..., 1:, :, :] - tile[..., :-1, :, :], jnp.zeros_like(tile[..., :1, :, :])], -3
    )
    grads = jnp.stack([dx[:, 0], dy[:, 0], dz[:, 0]], 1)
    dirs = jnp.stack([dx[:, 1], dy[:, 1], dz[:, 1]], 1)
    return (grads, dirs)


def moments(grads, dirs, weights):
    wts = weights[:, None, None, None]
    rows = [jnp.sum(wts * grads[:, i] * grads[:, j], 0) for i, j in SYM_PAIRS]
    for i in range(3):
        for j in range(3):
            rows.append(jnp.sum(wts * dirs[:, i] * grads[:, j], 0))
    return jnp.stack(rows, 0)


def couple(moms, grad_own, dir_own):
    trace_m = moms[0] + moms[1] + moms[2]
    mat = [[moms[0], moms[3], moms[4]], [moms[3], moms[1], moms[5]], [moms[4], moms[5], moms[2]]]
    nat = [[moms[6 + 3 * i + j] for j in range(3)] for i in range(3)]
    trace_n = nat[0][0] + nat[1][1] + nat[2][2]
    g_parts = [grad_own[..., i, :, :, :] for i in range(3)]
    e_parts = [dir_own[..., i, :, :, :] for i in range(3)]
    cross_q = []
    cross_p = []
    for i in range(3):
        mg = mat[i][0] * g_parts[0] + mat[i][1] * g_parts[1] + mat[i][2] * g_parts[2]
        me = mat[i][0] * e_parts[0] + mat[i][1] * e_parts[1] + mat[i][2] * e_parts[2]
        ng = nat[i][0] * g_parts[0] + nat[i][1] * g_parts[1] + nat[i][2] * g_parts[2]
        cross_q.append(trace_m * g_parts[i] - mg)
        cross_p.append(trace_m * e_parts[i] - me + trace_n * g_parts[i] - ng)
    return (jnp.stack(cross_q, axis=-4), jnp.stack(cross_p, axis=-4))


def model_split(every, rim_x, rim_y, alpha, beta, weights):
    grads, dirs = fields(every, rim_x, rim_y)
    moms = moments(grads, dirs, weights)
    grad_own = grads[0]
    dir_own = dirs[0]
    cross_q, cross_p = couple(moms, grad_own, dir_own)
    size = jnp.sqrt(jnp.sum(grad_own * grad_own, 0) + EPS_SQ)[None]
    flux = jnp.stack(
        [beta * grad_own / size + alpha * cross_q, beta * dir_own / size + alpha * cross_p], 0
    )
    last_x, last_y = edge_masks(flux.shape[3], flux.shape[4])
    flux_x = jnp.where(last_x, 0.0, flux[:, 0])
    flux_y = jnp.where(last_y, 0.0, flux[:, 1])
    levels = lax.broadcasted_iota(jnp.int32, (flux.shape[2], 1, 1), 0)
    flux_z = jnp.where(levels == flux.shape[2] - 1, 0.0, flux[:, 2])
    prev_y = passed_along(flux_y[..., -1:, :], "ty", 1)
    prev_x = lax.cond(
        lax.axis_index("mp") >= 0,
        lambda edge: passed_dense(edge, "tx", 1),
        jnp.zeros_like,
        flux_x[..., -1:],
    )

    def adjoint_one(out):
        fx, fy, fz = flux_x[out], flux_y[out], flux_z[out]
        res = jnp.concatenate([prev_x[out], fx[..., :-1]], -1) - fx
        res = res + jnp.concatenate([prev_y[out], fy[..., :-1, :]], -2) - fy
        below = jnp.where(levels == 0, 0.0, jnp.concatenate([fz[:1], fz[:-1]], 0))
        return (res + below - fz)[None]

    return (adjoint_one(0), adjoint_one(1))


def shards(models, direction, coupling, tv_weight):
    mp = lax.axis_size("mp")
    member = lax.axis_index("mp")
    local = models.shape[0]
    order = (member - jnp.arange(mp)) % mp
    picks = (order[:, None] * local + jnp.arange(local)[None, :]).reshape(-1)
    weights = jnp.take(coupling, picks)
    alpha = weights[0]
    beta = jnp.take(tv_weight, picks[:1])[0]
    own = jnp.stack([models, direction], 1)
    rim_x = passed_dense(own[..., :1], "tx", -1)
    rim_y = passed_along(own[..., :1, :], "ty", -1)
    rims = jnp.concatenate([rim_x.reshape(-1), rim_y.reshape(-1)])
    rims = rims.reshape(-1, 128) if rims.size % 128 == 0 else rims
    tiles, rims_x, rims_y = [own], [rim_x], [rim_y]
    for shift in range(1, mp):
        pairs = [(m, (m + shift) % mp) for m in range(mp)]
        tiles.append(lax.ppermute(own, "mp", pairs))
        theirs = lax.ppermute(rims, "mp", pairs).reshape(-1)
        rims_x.append(theirs[: rim_x.size].reshape(rim_x.shape))
        rims_y.append(theirs[rim_x.size :].reshape(rim_y.shape))
    every = jnp.concatenate(tiles, 0)
    rim_x = jnp.concatenate(rims_x, 0)
    rim_y = jnp.concatenate(rims_y, 0)
    return model_split(every, rim_x, rim_y, alpha, beta, weights)


def solution(mesh):
    placed = (P("mp", None, "ty", "tx"), P("mp", None, "ty", "tx"), P(), P())
    return jax.shard_map(
        shards,
        mesh=mesh,
        in_specs=placed,
        out_specs=(P("mp", None, "ty", "tx"), P("mp", None, "ty", "tx")),
        check_vma=False,
    )
```

```python
import jax
import jax.numpy as jnp
from jax import lax
from jax.sharding import PartitionSpec as P

EPS_SQ = 0.25
SYM_PAIRS = ((0, 0), (1, 1), (2, 2), (0, 1), (0, 2), (1, 2))


def passed_along(array, axis, by):
    size = lax.axis_size(axis)
    pairs = [(i, i + by) for i in range(size) if 0 <= i + by < size]
    return lax.ppermute(array, axis, pairs)


def passed_dense(array, axis, by):
    count = array.size
    rows = array.reshape(count // 128, 128) if count % 128 == 0 else array.reshape(count)
    return passed_along(rows, axis, by).reshape(array.shape)


def edge_masks(width_y, width_x):
    end_x = lax.axis_index("tx") == lax.axis_size("tx") - 1
    end_y = lax.axis_index("ty") == lax.axis_size("ty") - 1
    col_x = lax.broadcasted_iota(jnp.int32, (1, 1, width_x), 2)
    row_y = lax.broadcasted_iota(jnp.int32, (1, width_y, 1), 1)
    return ((col_x == width_x - 1) & end_x, (row_y == width_y - 1) & end_y)


def fields(tile, rim_x, rim_y):
    last_x, last_y = edge_masks(tile.shape[3], tile.shape[4])
    dx = jnp.concatenate([tile[..., 1:], rim_x], -1) - tile
    dx = jnp.where(last_x, 0.0, dx)
    dy = jnp.concatenate([tile[..., 1:, :], rim_y], -2) - tile
    dy = jnp.where(last_y, 0.0, dy)
    dz = jnp.concatenate(
        [tile[..., 1:, :, :] - tile[..., :-1, :, :], jnp.zeros_like(tile[..., :1, :, :])], -3
    )
    grads = jnp.stack([dx[:, 0], dy[:, 0], dz[:, 0]], 1)
    dirs = jnp.stack([dx[:, 1], dy[:, 1], dz[:, 1]], 1)
    return (grads, dirs)


def moments(grads, dirs, weights):
    wts = weights[:, None, None, None]
    rows = [jnp.sum(wts * grads[:, i] * grads[:, j], 0) for i, j in SYM_PAIRS]
    for i in range(3):
        for j in range(3):
            rows.append(jnp.sum(wts * dirs[:, i] * grads[:, j], 0))
    return jnp.stack(rows, 0)


def couple(moms, grad_own, dir_own):
    trace_m = moms[0] + moms[1] + moms[2]
    mat = [[moms[0], moms[3], moms[4]], [moms[3], moms[1], moms[5]], [moms[4], moms[5], moms[2]]]
    nat = [[moms[6 + 3 * i + j] for j in range(3)] for i in range(3)]
    trace_n = nat[0][0] + nat[1][1] + nat[2][2]
    g_parts = [grad_own[..., i, :, :, :] for i in range(3)]
    e_parts = [dir_own[..., i, :, :, :] for i in range(3)]
    cross_q = []
    cross_p = []
    for i in range(3):
        mg = mat[i][0] * g_parts[0] + mat[i][1] * g_parts[1] + mat[i][2] * g_parts[2]
        me = mat[i][0] * e_parts[0] + mat[i][1] * e_parts[1] + mat[i][2] * e_parts[2]
        ng = nat[i][0] * g_parts[0] + nat[i][1] * g_parts[1] + nat[i][2] * g_parts[2]
        cross_q.append(trace_m * g_parts[i] - mg)
        cross_p.append(trace_m * e_parts[i] - me + trace_n * g_parts[i] - ng)
    return (jnp.stack(cross_q, axis=-4), jnp.stack(cross_p, axis=-4))


def model_split(every, rim_x, rim_y, alpha, beta, weights):
    grads, dirs = fields(every, rim_x, rim_y)
    moms = moments(grads, dirs, weights)
    grad_own = grads[0]
    dir_own = dirs[0]
    cross_q, cross_p = couple(moms, grad_own, dir_own)
    size = jnp.sqrt(jnp.sum(grad_own * grad_own, 0) + EPS_SQ)[None]
    flux = jnp.stack(
        [beta * grad_own / size + alpha * cross_q, beta * dir_own / size + alpha * cross_p], 0
    )
    last_x, last_y = edge_masks(flux.shape[3], flux.shape[4])
    flux_x = jnp.where(last_x, 0.0, flux[:, 0])
    flux_y = jnp.where(last_y, 0.0, flux[:, 1])
    levels = lax.broadcasted_iota(jnp.int32, (flux.shape[2], 1, 1), 0)
    flux_z = jnp.where(levels == flux.shape[2] - 1, 0.0, flux[:, 2])
    prev_x = passed_dense(flux_x[..., -1:], "tx", 1)
    prev_y = passed_along(flux_y[..., -1:, :], "ty", 1)

    def adjoint_one(out):
        fx, fy, fz = flux_x[out], flux_y[out], flux_z[out]
        lane = lax.broadcasted_iota(jnp.int32, (1, 1, fx.shape[-1]), 2)
        row = lax.broadcasted_iota(jnp.int32, (1, fy.shape[-2], 1), 1)
        left = jnp.pad(fx[..., :-1], ((0, 0), (0, 0), (1, 0)))
        left = jnp.where(lane == 0, prev_x[out], left)
        above = jnp.pad(fy[..., :-1, :], ((0, 0), (1, 0), (0, 0)))
        above = jnp.where(row == 0, prev_y[out], above)
        res = left - fx
        res = res + above - fy
        below = jnp.where(levels == 0, 0.0, jnp.concatenate([fz[:1], fz[:-1]], 0))
        return (res + below - fz)[None]

    return (adjoint_one(0), adjoint_one(1))


def shards(models, direction, coupling, tv_weight):
    mp = lax.axis_size("mp")
    member = lax.axis_index("mp")
    local = models.shape[0]
    order = (member - jnp.arange(mp)) % mp
    picks = (order[:, None] * local + jnp.arange(local)[None, :]).reshape(-1)
    weights = jnp.take(coupling, picks)
    alpha = weights[0]
    beta = jnp.take(tv_weight, picks[:1])[0]
    own = jnp.stack([models, direction], 1)
    rim_x = passed_dense(own[..., :1], "tx", -1)
    rim_y = passed_along(own[..., :1, :], "ty", -1)
    rims = jnp.concatenate([rim_x.reshape(-1), rim_y.reshape(-1)])
    rims = rims.reshape(-1, 128) if rims.size % 128 == 0 else rims
    tiles, rims_x, rims_y = [own], [rim_x], [rim_y]
    for shift in range(1, mp):
        pairs = [(m, (m + shift) % mp) for m in range(mp)]
        tiles.append(lax.ppermute(own, "mp", pairs))
        theirs = lax.ppermute(rims, "mp", pairs).reshape(-1)
        rims_x.append(theirs[: rim_x.size].reshape(rim_x.shape))
        rims_y.append(theirs[rim_x.size :].reshape(rim_y.shape))
    every = jnp.concatenate(tiles, 0)
    rim_x = jnp.concatenate(rims_x, 0)
    rim_y = jnp.concatenate(rims_y, 0)
    return model_split(every, rim_x, rim_y, alpha, beta, weights)


def solution(mesh):
    placed = (P("mp", None, "ty", "tx"), P("mp", None, "ty", "tx"), P(), P())
    return jax.shard_map(
        shards,
        mesh=mesh,
        in_specs=placed,
        out_specs=(P("mp", None, "ty", "tx"), P("mp", None, "ty", "tx")),
        check_vma=False,
    )
```

```python
import jax
import jax.numpy as jnp
from jax import lax
from jax.sharding import PartitionSpec as P

EPS_SQ = 0.25
SYM_PAIRS = ((0, 0), (1, 1), (2, 2), (0, 1), (0, 2), (1, 2))


def passed_along(array, axis, by):
    size = lax.axis_size(axis)
    pairs = [(i, i + by) for i in range(size) if 0 <= i + by < size]
    return lax.ppermute(array, axis, pairs)


def passed_dense(array, axis, by):
    count = array.size
    rows = array.reshape(count // 128, 128) if count % 128 == 0 else array.reshape(count)
    return passed_along(rows, axis, by).reshape(array.shape)


def edge_masks(width_y, width_x):
    end_x = lax.axis_index("tx") == lax.axis_size("tx") - 1
    end_y = lax.axis_index("ty") == lax.axis_size("ty") - 1
    col_x = lax.broadcasted_iota(jnp.int32, (1, 1, width_x), 2)
    row_y = lax.broadcasted_iota(jnp.int32, (1, width_y, 1), 1)
    return ((col_x == width_x - 1) & end_x, (row_y == width_y - 1) & end_y)


def fields(tile, rim_x, rim_y):
    last_x, last_y = edge_masks(tile.shape[3], tile.shape[4])
    dx = jnp.concatenate([tile[..., 1:], rim_x], -1) - tile
    dx = jnp.where(last_x, 0.0, dx)
    dy = jnp.concatenate([tile[..., 1:, :], rim_y], -2) - tile
    dy = jnp.where(last_y, 0.0, dy)
    dz = jnp.concatenate(
        [tile[..., 1:, :, :] - tile[..., :-1, :, :], jnp.zeros_like(tile[..., :1, :, :])], -3
    )
    grads = jnp.stack([dx[:, 0], dy[:, 0], dz[:, 0]], 1)
    dirs = jnp.stack([dx[:, 1], dy[:, 1], dz[:, 1]], 1)
    return (grads, dirs)


def moments(grads, dirs, weights):
    wts = weights[:, None, None, None]
    rows = [jnp.sum(wts * grads[:, i] * grads[:, j], 0) for i, j in SYM_PAIRS]
    for i in range(3):
        for j in range(3):
            rows.append(jnp.sum(wts * dirs[:, i] * grads[:, j], 0))
    return jnp.stack(rows, 0)


def couple(moms, grad_own, dir_own):
    trace_m = moms[0] + moms[1] + moms[2]
    mat = [[moms[0], moms[3], moms[4]], [moms[3], moms[1], moms[5]], [moms[4], moms[5], moms[2]]]
    nat = [[moms[6 + 3 * i + j] for j in range(3)] for i in range(3)]
    trace_n = nat[0][0] + nat[1][1] + nat[2][2]
    g_parts = [grad_own[..., i, :, :, :] for i in range(3)]
    e_parts = [dir_own[..., i, :, :, :] for i in range(3)]
    cross_q = []
    cross_p = []
    for i in range(3):
        mg = mat[i][0] * g_parts[0] + mat[i][1] * g_parts[1] + mat[i][2] * g_parts[2]
        me = mat[i][0] * e_parts[0] + mat[i][1] * e_parts[1] + mat[i][2] * e_parts[2]
        ng = nat[i][0] * g_parts[0] + nat[i][1] * g_parts[1] + nat[i][2] * g_parts[2]
        cross_q.append(trace_m * g_parts[i] - mg)
        cross_p.append(trace_m * e_parts[i] - me + trace_n * g_parts[i] - ng)
    return (jnp.stack(cross_q, axis=-4), jnp.stack(cross_p, axis=-4))


def model_split(every, rim_x, rim_y, alpha, beta, weights):
    grads, dirs = fields(every, rim_x, rim_y)
    moms = moments(grads, dirs, weights)
    grad_own = grads[0]
    dir_own = dirs[0]
    cross_q, cross_p = couple(moms, grad_own, dir_own)
    size = jnp.sqrt(jnp.sum(grad_own * grad_own, 0) + EPS_SQ)[None]
    flux = jnp.stack(
        [beta * grad_own / size + alpha * cross_q, beta * dir_own / size + alpha * cross_p], 0
    )
    last_x, last_y = edge_masks(flux.shape[3], flux.shape[4])
    flux_x = jnp.where(last_x, 0.0, flux[:, 0])
    flux_y = jnp.where(last_y, 0.0, flux[:, 1])
    levels = lax.broadcasted_iota(jnp.int32, (flux.shape[2], 1, 1), 0)
    flux_z = jnp.where(levels == flux.shape[2] - 1, 0.0, flux[:, 2])
    prev_x = passed_dense(flux_x[..., -1:], "tx", 1)
    prev_y = passed_along(flux_y[..., -1:, :], "ty", 1)

    def adjoint_one(out):
        fx, fy, fz = flux_x[out], flux_y[out], flux_z[out]
        res = jnp.concatenate([prev_x[out], fx[..., :-1]], -1) - fx
        res = res + jnp.concatenate([prev_y[out], fy[..., :-1, :]], -2) - fy
        below = jnp.where(levels == 0, 0.0, jnp.concatenate([fz[:1], fz[:-1]], 0))
        return (res + below - fz)[None]

    return (adjoint_one(0), adjoint_one(1))


def shards(models, direction, coupling, tv_weight):
    mp = lax.axis_size("mp")
    member = lax.axis_index("mp")
    local = models.shape[0]
    order = (member - jnp.arange(mp)) % mp
    picks = (order[:, None] * local + jnp.arange(local)[None, :]).reshape(-1)
    values = jnp.take(jnp.concatenate([coupling, tv_weight]), jnp.append(picks, picks[0] + coupling.size))
    weights = values[:-1]
    alpha = weights[0]
    beta = values[-1]
    own = jnp.stack([models, direction], 1)
    rim_x = passed_dense(own[..., :1], "tx", -1)
    rim_y = passed_along(own[..., :1, :], "ty", -1)
    rims = jnp.concatenate([rim_x.reshape(-1), rim_y.reshape(-1)])
    rims = rims.reshape(-1, 128) if rims.size % 128 == 0 else rims
    tiles, rims_x, rims_y = [own], [rim_x], [rim_y]
    for shift in range(1, mp):
        pairs = [(m, (m + shift) % mp) for m in range(mp)]
        tiles.append(lax.ppermute(own, "mp", pairs))
        theirs = lax.ppermute(rims, "mp", pairs).reshape(-1)
        rims_x.append(theirs[: rim_x.size].reshape(rim_x.shape))
        rims_y.append(theirs[rim_x.size :].reshape(rim_y.shape))
    every = jnp.concatenate(tiles, 0)
    rim_x = jnp.concatenate(rims_x, 0)
    rim_y = jnp.concatenate(rims_y, 0)
    return model_split(every, rim_x, rim_y, alpha, beta, weights)


def solution(mesh):
    placed = (P("mp", None, "ty", "tx"), P("mp", None, "ty", "tx"), P(), P())
    return jax.shard_map(
        shards,
        mesh=mesh,
        in_specs=placed,
        out_specs=(P("mp", None, "ty", "tx"), P("mp", None, "ty", "tx")),
        check_vma=False,
    )
```
